128 devices in a mesh: req: 16 (over x, z), head: 8 (over y, core).
Axes of the slice: x: 4, y: 4, z: 4, core: 2. Of those that a mesh axis runs over, the one named last changes fastest.
Arguments:
- tokens: bfloat16 [16384, 1536], P('req', 'head'), may hold values from -6 to 6
- new_counts: int32 [16, 4], P('req'), may hold values from 1 to 512, 1024 in all within a row
- kv_cache: bfloat16 [64, 8, 7680, 128], P('req', 'head'), may hold values from -300 to 300
- norm_attn: float32 [1536], replicated, may hold values from 0.1 to 1.9
- query_weight: bfloat16 [1536, 8, 192], P(None, 'head'), may hold values from -0.15625 to 0.15625
- key_value_weight: bfloat16 [1536, 8, 128], P(None, 'head'), may hold values from -0.4375 to 0.4375
- output_weight: bfloat16 [8, 192, 1536], P('head'), may hold values from -0.15625 to 0.15625
- norm_moe: float32 [1536], replicated, may hold values from 0.1 to 1.9
- routes: int32 [16384, 8], P(('req', 'head')), may hold values from 0 to 31, all different within a row; in each aligned block of 128 rows (0 to 127, 128 to 255, ...) at most 64 rows name the same one
- route_gain: float32 [16384, 8], P(('req', 'head')), may hold values from 0.03 to 0.3
- w_gate_up: bfloat16 [32, 1536, 1024], P('req'), may hold values from -0.15625 to 0.15625
- w_down: bfloat16 [32, 512, 1536], P('req'), may hold values from -0.25 to 0.25
Outputs:
- mixed: bfloat16 [16384, 1536], P(('req', 'head'))
The draws below stay inside these ranges and needn't reach their ends.
Inputs may be any that keep to these rules, and one draw needn't show every extreme that they name: `new_counts`: the 4 counts of one index of req sum to 1024, and one of them is exactly 512. `routes`: the 8 experts of a row differ. In each aligned block of 128 rows (the rows of one device) no expert is named more than 64 times, a bound that some block reaches.
All inputs are finite; a program needn't handle non-finite values.
Results may differ from the reference program's by a relative error of at most 0.019.
Values may be sent and summed in bfloat16 or wider, within the bound.
No kernel may reach another device: no remote copies, remote signals or barrier semaphores. Data moves between devices by JAX's collectives and lax.ppermute only.
A program may use at most 128 MiB of HBM per device.

```python
import math
import jax
import jax.numpy as jnp
import numpy as np
from jax import lax

MODEL_DIM = 1536
QUERY_HEADS = 24
KEY_HEADS = 8
HEAD_DIM = 64
FF = 512
EXPERTS = 32
TOPK = 8
RATIO = 15
REQ_DEV = 4
TOK_DEV = 1024
QUERY_PER_KV = 3
MOSTN = 512
CACHE_SLOTS = 7680
MT = 128
CAP = 64
TOKENS = 16384
REQUEST_TOTAL = 64
N_HEAD = 8


def draw_kv_cache(key, part):
    key_primary = jax.random.fold_in(key, 11)
    value_rows = jnp.clip(jax.random.normal(key_primary, (REQUEST_TOTAL, KEY_HEADS, CACHE_SLOTS, 2 * HEAD_DIM), jnp.float32), -6.0, 6.0)
    key_scaling = jnp.full((REQUEST_TOTAL, KEY_HEADS, CACHE_SLOTS, 1), 2.5, jnp.float32)
    scaled = jnp.concatenate([value_rows[..., :HEAD_DIM] * key_scaling, value_rows[..., HEAD_DIM:]], axis=3)
    return scaled.astype(jnp.bfloat16)


def steps_of(own_key, extent, cuts, least, high):
    def one(axis_at, parts):
        steps = jax.random.uniform(jax.random.fold_in(jax.random.fold_in(own_key, 6), axis_at), (parts,), jnp.float32, least / len(cuts), high / len(cuts))
        return jnp.repeat(jnp.exp(steps), extent[axis_at] // parts).reshape((-1,) + (1,) * (len(extent) - axis_at - 1))

    gain = one(*cuts[0])
    for cut in cuts[1:]:
        gain = gain * one(*cut)
    return gain


def split_up(amount, total, reach, skew):
    loads = [(1 << 20) // math.isqrt(standing ** skew) + 1 for standing in range(2, amount + 1)]
    spare, given = total - reach - (amount - 1), [1] * (amount - 1)
    while spare > 0:
        free = [i for i in range(amount - 1) if given[i] < reach]
        whole, left = sum([loads[i] for i in free]), spare
        for i in free:
            more = min(reach - given[i], max(1, left * loads[i] // whole), spare)
            given[i] = given[i] + more
            spare = spare - more
    return np.array([reach] + given)


def uneven(key, count, total, limit, slope):
    if count == 2:
        one = jax.random.randint(key, (), max(1, total - limit), min(limit, total - 1) + 1)
        return jnp.stack([one, total - one])
    lengths = jnp.asarray(split_up(count, total, limit, slope), jnp.int32)
    pairs = (count - 1) // 2
    source_of, taker = lengths[1:1 + 2 * pairs:2], lengths[2:2 + 2 * pairs:2]
    margin = jnp.minimum(source_of - 1, limit - taker)
    shifted = jax.random.randint(jax.random.fold_in(key, 1), (pairs,), 0, 1 << 20) % (margin + 1)
    lengths = lengths.at[1:1 + 2 * pairs:2].set(source_of - shifted).at[2:2 + 2 * pairs:2].set(taker + shifted)
    return lengths[jax.random.permutation(jax.random.fold_in(key, 2), count)]


def routed_block(rng, own, number, rows, count, top, limit, skew):
    ranking = jax.random.permutation(rng, count)
    crowded, usual = portions_of(count, rows * top, limit, skew, True), portions_of(count, rows * top, limit, skew, False)
    places = jnp.arange(count)

    def named(sizes, offset_by):
        used = int((sizes > 0).sum())
        fixed = max(1, used // 4)
        shifted = fixed + (places - fixed + offset_by * (used - fixed)) % max(1, count - fixed)
        return jnp.zeros((count,), jnp.int32).at[ranking[jnp.where(places < fixed, places, shifted)]].set(jnp.asarray(sizes, jnp.int32))

    sizes = jnp.where(number % 4 == 0, named(crowded, number // 4), named(usual, number - number // 4 - 1))
    mixed = jax.random.permutation(jax.random.fold_in(own, 3), count)
    source_of, taker = mixed[0:count // 2 * 2:2], mixed[1:count // 2 * 2:2]
    margin = jnp.minimum(sizes[source_of] - 1, limit - sizes[taker]) // 2
    margin = jnp.where((source_of == ranking[0]) | (taker == ranking[0]) | (sizes[taker] == 0), 0, jnp.maximum(margin, 0))
    shifted = jax.random.randint(jax.random.fold_in(own, 4), (count // 2,), 0, 1 << 20) % (margin + 1)
    sizes = sizes.at[source_of].add(-shifted).at[taker].add(shifted)
    items = jnp.searchsorted(jnp.cumsum(sizes), jnp.arange(rows * top), side="right").astype(jnp.int32)
    grid = items.reshape(top, rows).T
    grid = grid[jax.random.permutation(jax.random.fold_in(own, 1), rows)]
    offset_by = jax.random.randint(jax.random.fold_in(own, 2), (rows, 1), 0, top)
    return jnp.take_along_axis(grid, (jnp.arange(top)[None, :] + offset_by) % top, axis=1)


def portions_of(amount, total, bound, slope, full):
    portions = [(1 << 20) // math.isqrt(rank ** slope) + 1 for rank in range(1, amount + 1)]
    largest = bound if full else min(bound, max(-(-total // amount), total * portions[0] // sum(portions)))
    least = 1 if total - largest >= amount - 1 else 0
    given, surplus = [largest] + [least] * (amount - 1), total - largest - least * (amount - 1)
    while surplus > 0:
        movable = [i for i in range(1, amount) if given[i] < largest] or [i for i in range(1, amount) if given[i] < bound]
        whole, left = sum([portions[i] for i in movable]), surplus
        for i in movable:
            more = min(bound - given[i], max(1, left * portions[i] // whole), surplus)
            given[i] = given[i] + more
            surplus = surplus - more
    return np.array(given)


def scatter_about(own_key, extent, scale, reach, shards=(), kind=jnp.bfloat16):
    values = jax.random.normal(own_key, extent, jnp.float32) * scale
    if len(shards) > 0:
        values = steps_of(own_key, extent, shards, -0.22, 0.18) * values
    return jnp.clip(values, min=-reach, max=reach).astype(kind)


def setup_inputs(seed: int = 0) -> dict:
    splits = jax.random.split(jax.random.key(seed), 13)
    tokens = scatter_about(splits[0], (TOKENS, MODEL_DIM), 1.0, 6.0, ((0, 16), (1, 8)))
    new_counts = jax.vmap(lambda own: uneven(own, REQ_DEV, TOK_DEV, MOSTN, 2))(jax.random.split(splits[1], (REQUEST_TOTAL // REQ_DEV))).reshape((REQUEST_TOTAL // REQ_DEV, REQ_DEV)).astype(jnp.int32)
    kv_cache = draw_kv_cache(jax.random.fold_in(splits[12], 71), 0)
    norm_attn = jnp.clip(1.0 + 0.18 * jax.random.normal(splits[3], (MODEL_DIM,), jnp.float32), 0.1, 1.9)
    query_weight = scatter_about(splits[4], (MODEL_DIM, KEY_HEADS, QUERY_PER_KV * HEAD_DIM), MODEL_DIM ** -0.5, 0.15625, ((1, 8),))
    key_value_weight = scatter_about(splits[5], (MODEL_DIM, KEY_HEADS, 2 * HEAD_DIM), (MODEL_DIM // 9) ** -0.5, 0.4375, ((1, 8),))
    output_weight = scatter_about(splits[6], (KEY_HEADS, QUERY_PER_KV * HEAD_DIM, MODEL_DIM), (QUERY_HEADS * HEAD_DIM) ** -0.5, 0.15625, ((0, 8),))
    norm_moe = jnp.clip(1.0 + 0.18 * jax.random.normal(splits[7], (MODEL_DIM,), jnp.float32), 0.1, 1.9)
    routes_keys = jax.random.split(jax.random.fold_in(splits[8], 1), TOKENS // MT)
    routes_turns = jax.random.permutation(jax.random.fold_in(splits[8], 3), TOKENS // MT)
    routes = jax.vmap(lambda own, number: routed_block(jax.random.fold_in(splits[8], 2), own, number, MT, EXPERTS, TOPK, CAP, 2))(routes_keys, routes_turns).reshape((TOKENS, TOPK))
    route_gain = jnp.clip(jnp.exp(math.log(0.3) - 2.3025852 * jax.random.uniform(splits[9], (TOKENS, TOPK), jnp.float32) ** steps_of(splits[9], (TOKENS, TOPK), ((0, 128),), -0.2, 0.2)), 0.03, 0.3)
    w_gate_up = scatter_about(splits[10], (EXPERTS, MODEL_DIM, 2 * FF), MODEL_DIM ** -0.5, 0.15625, ((0, 16),))
    w_down = scatter_about(splits[11], (EXPERTS, FF, MODEL_DIM), FF ** -0.5, 0.25, ((0, 16),))
    return dict(tokens=tokens, new_counts=new_counts, kv_cache=kv_cache, norm_attn=norm_attn, query_weight=query_weight, key_value_weight=key_value_weight, output_weight=output_weight, norm_moe=norm_moe, routes=routes, route_gain=route_gain, w_gate_up=w_gate_up, w_down=w_down)


floor_score = -1e+30

def norm_rows(value_rows, gain_row):
    mean_square = lax.optimization_barrier(jnp.mean(value_rows * value_rows, axis=-1, keepdims=True))
    return value_rows * lax.rsqrt(mean_square + 1e-05) * gain_row

def rope_tables(position, head_size):
    half_size = head_size // 2
    inverse = jnp.exp(jnp.arange(half_size, dtype=jnp.float32) * (-2.0 * math.log(10000.0) / head_size))
    angles = position.astype(jnp.float32)[:, None] * inverse[None, :]
    angles = jnp.concatenate([angles, angles], axis=1)
    return (jnp.cos(angles), jnp.sin(angles))

def rotate(vectors, cos_part, sin_part):
    half_size = vectors.shape[-1] // 2
    turned = jnp.concatenate([-vectors[..., half_size:], vectors[..., :half_size]], axis=-1)
    return vectors * cos_part + turned * sin_part

def request_layout(counts, token_count, cache_ratio):
    counts = counts.astype(jnp.int32)
    end_rows = jnp.cumsum(counts).astype(jnp.int32)
    starts = (end_rows - counts).astype(jnp.int32)
    row_ids = jnp.arange(token_count, dtype=jnp.int32)
    segment = lax.optimization_barrier(jnp.sum((row_ids[:, None] >= end_rows[None, :]).astype(jnp.int32), axis=1)).astype(jnp.int32)
    member = (segment[:, None] == jnp.arange(counts.shape[0], dtype=jnp.int32)[None, :]).astype(jnp.int32)
    row_begin = lax.optimization_barrier(jnp.sum(member * starts[None, :], axis=1)).astype(jnp.int32)
    own_count = lax.optimization_barrier(jnp.sum(member * counts[None, :], axis=1)).astype(jnp.int32)
    position = (cache_ratio * own_count + row_ids - row_begin).astype(jnp.int32)
    return (starts, position)

def project(normed, query_weight, key_value_weight, position):
    token_count, model_width = normed.shape
    kv_heads = key_value_weight.shape[1]
    head_size = key_value_weight.shape[2] // 2
    group_size = query_weight.shape[2] // head_size
    query = jnp.dot(normed, query_weight.reshape(model_width, -1), preferred_element_type=jnp.float32)
    query = query.reshape(token_count, kv_heads, group_size, head_size)
    keyval = jnp.dot(normed, key_value_weight.reshape(model_width, -1), preferred_element_type=jnp.float32)
    keyval = keyval.reshape(token_count, kv_heads, 2 * head_size)
    cos_part, sin_part = rope_tables(position, head_size)
    query = rotate(query, cos_part[:, None, None, :], sin_part[:, None, None, :]).astype(jnp.bfloat16)
    new_key = rotate(keyval[..., :head_size], cos_part[:, None, :], sin_part[:, None, :]).astype(jnp.bfloat16)
    new_value = keyval[..., head_size:].astype(jnp.bfloat16)
    return (query, new_key, new_value)

def round_half(value_rows):
    return lax.optimization_barrier(value_rows.astype(jnp.bfloat16)).astype(jnp.float32)

def attend_group(normed, counts, cache, query_weight, key_value_weight):
    token_count = normed.shape[0]
    counts = counts.astype(jnp.int32)
    starts, position = request_layout(counts, token_count, RATIO)
    query, new_key, new_value = project(normed, query_weight, key_value_weight, position)
    head_size = new_key.shape[-1]
    window = token_count // 2
    score_scale = 1.0 / math.sqrt(head_size)
    cache_len = cache.shape[2]

    def one_request(which, result):
        row_begin = starts[which]
        count_here = counts[which]
        cached = RATIO * count_here
        win_start = jnp.minimum(row_begin, token_count - window).astype(jnp.int32)
        row_ids = win_start + jnp.arange(window, dtype=jnp.int32)
        inside = (row_ids >= row_begin) & (row_ids < row_begin + count_here)
        q_win = lax.dynamic_slice_in_dim(query, win_start, window, 0).astype(jnp.float32)
        k_win = lax.dynamic_slice_in_dim(new_key, win_start, window, 0).astype(jnp.float32)
        v_win = lax.dynamic_slice_in_dim(new_value, win_start, window, 0).astype(jnp.float32)
        p_win = lax.dynamic_slice_in_dim(position, win_start, window, 0)
        past = lax.dynamic_index_in_dim(cache, which, 0, keepdims=False).astype(jnp.float32)
        old_ok = (jnp.arange(cache_len, dtype=jnp.int32) < cached)[None, None, None, :]
        new_ok = (inside[None, :] & (p_win[None, :] <= p_win[:, None]))[None, None, :, :]
        old_score = jnp.einsum('qhgd,hkd->hgqk', q_win, past[..., :head_size]) * score_scale
        new_score = jnp.einsum('qhgd,khd->hgqk', q_win, k_win) * score_scale
        old_score = jnp.where(old_ok, old_score, floor_score)
        new_score = jnp.where(new_ok, new_score, floor_score)
        highest = jnp.maximum(lax.optimization_barrier(jnp.max(old_score, axis=-1)), lax.optimization_barrier(jnp.max(new_score, axis=-1)))[..., None]
        old_exp = jnp.where(old_ok, jnp.exp(old_score - highest), 0.0)
        new_exp = jnp.where(new_ok, jnp.exp(new_score - highest), 0.0)
        denominator = lax.optimization_barrier(jnp.sum(old_exp, axis=-1)) + lax.optimization_barrier(jnp.sum(new_exp, axis=-1))
        numerator = jnp.einsum('hgqk,hkd->hgqd', round_half(old_exp), past[..., head_size:])
        numerator = numerator + jnp.einsum('hgqk,khd->hgqd', round_half(new_exp), v_win)
        attended = jnp.transpose(numerator / denominator[..., None], (2, 0, 1, 3))
        current = lax.dynamic_slice_in_dim(result, win_start, window, 0)
        update = jnp.where(inside[:, None, None, None], attended, current)
        return lax.dynamic_update_slice_in_dim(result, update, win_start, 0)
    initial = jnp.zeros(query.shape, jnp.float32)
    result = lax.fori_loop(0, counts.shape[0], one_request, initial)
    return result.astype(jnp.bfloat16)

def reference(tokens, new_counts, kv_cache, norm_attn, query_weight, key_value_weight, output_weight, norm_moe, routes, route_gain, w_gate_up, w_down):
    model_width = tokens.shape[1]
    groups = new_counts.shape[0]
    tok_groups = tokens.reshape(groups, TOK_DEV, model_width)
    cache_groups = kv_cache.reshape((groups, REQ_DEV) + kv_cache.shape[1:])
    out_blocks = output_weight.reshape(N_HEAD, -1, model_width).astype(jnp.float32)

    def group_step(inputs):
        tok_part, count_part, cache_part = inputs
        normed = norm_rows(tok_part.astype(jnp.float32), norm_attn).astype(jnp.bfloat16)
        attended = attend_group(normed, count_part, cache_part, query_weight, key_value_weight)
        flat_out = attended.reshape(TOK_DEV, N_HEAD, -1).astype(jnp.float32)
        partials = jnp.einsum('tjc,jcd->jtd', flat_out, out_blocks).astype(jnp.bfloat16)
        return tok_part.astype(jnp.float32) + lax.optimization_barrier(jnp.sum(partials.astype(jnp.float32), axis=0))
    resid = lax.map(group_step, (tok_groups, new_counts, cache_groups)).reshape(-1, model_width)
    moe_in = norm_rows(resid, norm_moe).astype(jnp.bfloat16)
    token_total = moe_in.shape[0]
    per_block = TOK_DEV // N_HEAD
    capacity = per_block // 2
    block_total = token_total // per_block
    route_blocks = routes.reshape(block_total, per_block * TOPK).astype(jnp.int32)
    expert_ids = jnp.arange(EXPERTS, dtype=jnp.int32)

    def slot_of(route_row):
        onehot = (route_row[:, None] == expert_ids[None, :]).astype(jnp.int32)
        before = (jnp.cumsum(onehot, axis=0) - onehot).astype(jnp.int32)
        rank_in = lax.optimization_barrier(jnp.sum(before * onehot, axis=1)).astype(jnp.int32)
        return (route_row * capacity + rank_in).astype(jnp.int32)
    slot_ids = jax.vmap(slot_of)(route_blocks)
    owners = jnp.arange(per_block * TOPK, dtype=jnp.int32) // TOPK

    def table_of(slot_row):
        return jnp.full((EXPERTS * capacity,), per_block, jnp.int32).at[slot_row].set(owners)
    tables = jax.vmap(table_of)(slot_ids)
    block_base = (jnp.arange(block_total, dtype=jnp.int32) * per_block)[:, None]
    token_slot = slot_ids.reshape(token_total, TOPK)
    token_block = jnp.arange(token_total, dtype=jnp.int32) // per_block
    ff_width = w_down.shape[1]

    def expert_step(running, expert):
        fill_ids = lax.dynamic_slice_in_dim(tables, expert * capacity, capacity, 1)
        present = (fill_ids < per_block).reshape(-1)
        source = (block_base + jnp.minimum(fill_ids, per_block - 1)).reshape(-1).astype(jnp.int32)
        picked = jnp.where(present[:, None], moe_in[source], jnp.zeros((), moe_in.dtype))
        gate_up = jnp.dot(picked, w_gate_up[expert], preferred_element_type=jnp.float32)
        hidden = (jax.nn.silu(gate_up[:, :ff_width]) * gate_up[:, ff_width:]).astype(jnp.bfloat16)
        produced = jnp.dot(hidden, w_down[expert], preferred_element_type=jnp.float32).astype(jnp.bfloat16)
        chosen = routes == expert
        rank_in = lax.optimization_barrier(jnp.sum(jnp.where(chosen, token_slot - expert * capacity, 0), axis=1)).astype(jnp.int32)
        weight = lax.optimization_barrier(jnp.sum(jnp.where(chosen, route_gain, 0.0), axis=1))
        gathered = produced[(token_block * capacity + rank_in).astype(jnp.int32)].astype(jnp.float32)
        return (running + weight[:, None] * gathered, None)
    moe_sum, _ = lax.scan(expert_step, jnp.zeros(resid.shape, jnp.float32), expert_ids)
    return (resid + moe_sum).astype(jnp.bfloat16)
```

```python
import math

import jax
import jax.numpy as jnp
from jax import lax
from jax.experimental import pallas as pl
from jax.experimental.pallas import tpu as pltpu
from jax.sharding import PartitionSpec as P

EXPERTS = 32
TOPK = 8
RATIO = 15
WIN = 512
TQ = 256
TK = 1536


floor_score = -1e30


def norm_rows(value_rows, gain_row):
    mean_square = jnp.mean(value_rows * value_rows, axis=-1, keepdims=True)
    return value_rows * lax.rsqrt(mean_square + 1e-05) * gain_row


def rope_tables(position, head_size):
    half_size = head_size // 2
    inverse = jnp.exp(
        jnp.arange(half_size, dtype=jnp.float32) * (-2.0 * math.log(10000.0) / head_size)
    )
    angles = position.astype(jnp.float32)[:, None] * inverse[None, :]
    angles = jnp.concatenate([angles, angles], axis=1)
    return (jnp.cos(angles), jnp.sin(angles))


def rotate(vectors, cos_part, sin_part):
    half_size = vectors.shape[-1] // 2
    turned = jnp.concatenate([-vectors[..., half_size:], vectors[..., :half_size]], axis=-1)
    return vectors * cos_part + turned * sin_part


def request_layout(counts, token_count, cache_ratio):
    end_rows = jnp.cumsum(counts)
    starts = end_rows - counts
    row_ids = jnp.arange(token_count, dtype=jnp.int32)
    segment = jnp.sum((row_ids[:, None] >= end_rows[None, :]).astype(jnp.int32), axis=1)
    member = (segment[:, None] == jnp.arange(counts.shape[0], dtype=jnp.int32)[None, :]).astype(
        jnp.int32
    )
    row_begin = jnp.sum(member * starts[None, :], axis=1)
    own_count = jnp.sum(member * counts[None, :], axis=1)
    position = cache_ratio * own_count + row_ids - row_begin
    return (starts, position)


def project(normed, query_weight, key_value_weight, position):
    token_count, model_width = normed.shape
    kv_heads = key_value_weight.shape[1]
    head_size = key_value_weight.shape[2] // 2
    group_size = query_weight.shape[2] // head_size
    query = jnp.dot(
        normed, query_weight.reshape(model_width, -1), preferred_element_type=jnp.float32
    )
    query = query.reshape(token_count, kv_heads, group_size, head_size)
    keyval = jnp.dot(
        normed, key_value_weight.reshape(model_width, -1), preferred_element_type=jnp.float32
    )
    keyval = keyval.reshape(token_count, kv_heads, 2 * head_size)
    cos_part, sin_part = rope_tables(position, head_size)
    query = rotate(query, cos_part[:, None, None, :], sin_part[:, None, None, :]).astype(
        jnp.bfloat16
    )
    new_key = rotate(keyval[..., :head_size], cos_part[:, None, :], sin_part[:, None, :]).astype(
        jnp.bfloat16
    )
    new_value = keyval[..., head_size:].astype(jnp.bfloat16)
    return (query, new_key, new_value)


def attn_kernel(counts_ref, q_ref, kv_ref, nkv_ref, o_ref, m_sc, l_sc, acc_sc):
    j = pl.program_id(0)
    qi = pl.program_id(1)
    kb = pl.program_id(2)
    last = pl.num_programs(2) - 1
    count = counts_ref[j]
    groups, tq, width = q_ref.shape[1], q_ref.shape[2], q_ref.shape[3]
    tk = kv_ref.shape[2]
    win = nkv_ref.shape[1]
    scale = 1.0 / math.sqrt(width // 2)
    tile_ok = qi * tq < count

    @pl.when(kb == 0)
    def _():
        m_sc[...] = jnp.full(m_sc.shape, floor_score, jnp.float32)
        l_sc[...] = jnp.zeros(l_sc.shape, jnp.float32)
        acc_sc[...] = jnp.zeros(acc_sc.shape, jnp.float32)

    def absorb(rows, mask):
        q = q_ref[0].reshape(groups * tq, width)
        s = lax.dot_general(
            q, rows, (((1,), (1,)), ((), ())), preferred_element_type=jnp.float32
        )
        s = (s * scale).reshape(groups, tq, rows.shape[0])
        s = jnp.where(mask, s, floor_score)
        m_old = m_sc[...]
        m_new = jnp.maximum(m_old, jnp.max(s, axis=-1, keepdims=True))
        alpha = jnp.exp(m_old - m_new)
        p = jnp.where(mask, jnp.exp(s - m_new), 0.0)
        l_sc[...] = l_sc[...] * alpha + jnp.sum(p, axis=-1, keepdims=True)
        pv = jnp.dot(
            p.astype(jnp.bfloat16).reshape(groups * tq, rows.shape[0]),
            rows,
            preferred_element_type=jnp.float32,
        )
        acc_sc[...] = acc_sc[...] * alpha + pv.reshape(groups, tq, width)
        m_sc[...] = m_new

    @pl.when(tile_ok & (kb == 0))
    def _():
        row = qi * tq + lax.broadcasted_iota(jnp.int32, (1, tq, win), 1)
        col = lax.broadcasted_iota(jnp.int32, (1, tq, win), 2)
        absorb(nkv_ref[0], col <= row)

    @pl.when(tile_ok & (kb > 0) & ((kb - 1) * tk < RATIO * count))
    def _():
        col = (kb - 1) * tk + lax.broadcasted_iota(jnp.int32, (1, 1, tk), 2)
        absorb(kv_ref[0, 0], col < RATIO * count)

    @pl.when(kb == last)
    def _():
        total = l_sc[...]
        total = jnp.where(total > 0.0, total, 1.0)
        o_ref[0] = (acc_sc[...] / total).astype(o_ref.dtype)


def attention(counts, q_win, kv_cache, nkv_win):
    req_n, groups, win, width = q_win.shape
    cache_len = kv_cache.shape[2]
    n_tiles = win // TQ
    n_blocks = cache_len // TK

    def q_map(j, qi, kb, cnt):
        tiles = (cnt[j] + TQ - 1) // TQ
        return (j, 0, jnp.minimum(qi, tiles - 1), 0)

    def kv_map(j, qi, kb, cnt):
        tiles = (cnt[j] + TQ - 1) // TQ
        blocks = (RATIO * cnt[j] + TK - 1) // TK
        inner = jnp.clip(kb - 1, 0, blocks - 1)
        return (j, 0, jnp.where(qi < tiles, inner, blocks - 1), 0)

    grid_spec = pltpu.PrefetchScalarGridSpec(
        num_scalar_prefetch=1,
        grid=(req_n, n_tiles, n_blocks + 1),
        in_specs=[
            pl.BlockSpec((1, groups, TQ, width), q_map),
            pl.BlockSpec((1, 1, TK, width), kv_map),
            pl.BlockSpec((1, win, width), lambda j, qi, kb, cnt: (j, 0, 0)),
        ],
        out_specs=pl.BlockSpec((1, groups, TQ, width), lambda j, qi, kb, cnt: (j, 0, qi, 0)),
        scratch_shapes=[
            pltpu.VMEM((groups, TQ, 1), jnp.float32),
            pltpu.VMEM((groups, TQ, 1), jnp.float32),
            pltpu.VMEM((groups, TQ, width), jnp.float32),
        ],
    )
    return pl.pallas_call(
        attn_kernel,
        grid_spec=grid_spec,
        out_shape=jax.ShapeDtypeStruct(q_win.shape, jnp.bfloat16),
        compiler_params=pltpu.CompilerParams(
            dimension_semantics=("arbitrary", "arbitrary", "arbitrary")
        ),
    )(counts, q_win, kv_cache, nkv_win)


def local(
    tokens,
    new_counts,
    kv_cache,
    norm_attn,
    query_weight,
    key_value_weight,
    output_weight,
    norm_moe,
    routes,
    route_gain,
    w_gate_up,
    w_down,
):
    whole = lax.all_gather(tokens, "head", axis=1, tiled=True)
    token_count, model_width = whole.shape
    normed = norm_rows(whole.astype(jnp.float32), norm_attn).astype(jnp.bfloat16)
    counts = new_counts[0]
    starts, position = request_layout(counts, token_count, RATIO)
    query, new_key, new_value = project(normed, query_weight, key_value_weight, position)
    groups, head_size = query.shape[2], query.shape[3]
    req_n = counts.shape[0]
    width = 2 * head_size

    query = query.reshape(token_count, groups, head_size)
    query = jnp.concatenate([query, jnp.zeros_like(query)], axis=-1)
    query = jnp.concatenate([query, jnp.zeros((WIN,) + query.shape[1:], query.dtype)], axis=0)
    newkv = jnp.concatenate([new_key[:, 0], new_value[:, 0]], axis=-1)
    newkv = jnp.concatenate([newkv, jnp.zeros((WIN, width), newkv.dtype)], axis=0)
    q_win = jnp.stack(
        [lax.dynamic_slice_in_dim(query, starts[j], WIN, 0) for j in range(req_n)]
    )
    q_win = jnp.transpose(q_win, (0, 2, 1, 3))
    nkv_win = jnp.stack(
        [lax.dynamic_slice_in_dim(newkv, starts[j], WIN, 0) for j in range(req_n)]
    )
    out_win = attention(counts, q_win, kv_cache, nkv_win)
    out_win = jnp.transpose(out_win[..., head_size:], (0, 2, 1, 3)).reshape(
        req_n, WIN, groups * head_size
    )
    result = jnp.zeros((token_count + WIN, groups * head_size), jnp.bfloat16)
    for j in range(req_n):
        result = lax.dynamic_update_slice_in_dim(result, out_win[j], starts[j], 0)
    attn_out = result[:token_count]

    partial_value = jnp.dot(
        attn_out, output_weight.reshape(-1, model_width), preferred_element_type=jnp.float32
    )
    per_block = routes.shape[0]
    row_start = lax.axis_index("head") * per_block
    attn_rows = lax.psum_scatter(
        partial_value.astype(jnp.bfloat16), "head", scatter_dimension=0, tiled=True
    ).astype(jnp.float32)
    base_rows = lax.dynamic_slice_in_dim(whole, row_start, per_block, 0)
    resid = base_rows.astype(jnp.float32) + attn_rows
    moe_in = norm_rows(resid, norm_moe).astype(jnp.bfloat16)
    capacity = per_block // 2
    flat_routes = routes.reshape(-1)
    expert_ids = jnp.arange(EXPERTS, dtype=jnp.int32)
    onehot = (flat_routes[:, None] == expert_ids[None, :]).astype(jnp.int32)
    before = jnp.cumsum(onehot, axis=0) - onehot
    rank_in = jnp.sum(before * onehot, axis=1)
    slot_ids = flat_routes * capacity + rank_in
    owners = jnp.arange(per_block * TOPK, dtype=jnp.int32) // TOPK
    table = jnp.full((EXPERTS * capacity,), per_block, jnp.int32).at[slot_ids].set(owners)
    padded = jnp.concatenate([moe_in, jnp.zeros((1, model_width), jnp.bfloat16)], axis=0)
    req_count = lax.axis_size("req")
    per_req = w_down.shape[0]
    ff_width = w_down.shape[1]
    outgoing = padded[table].reshape(req_count, per_req, capacity, model_width)
    gate_up = jnp.einsum(
        "sncd,ndf->sncf",
        lax.all_to_all(outgoing, "req", split_axis=0, concat_axis=0, tiled=True),
        w_gate_up,
        preferred_element_type=jnp.float32,
    )
    hidden = (jax.nn.silu(gate_up[..., :ff_width]) * gate_up[..., ff_width:]).astype(jnp.bfloat16)
    produced = jnp.einsum(
        "sncf,nfd->sncd", hidden, w_down, preferred_element_type=jnp.float32
    ).astype(jnp.bfloat16)
    arrived = lax.all_to_all(produced, "req", split_axis=0, concat_axis=0, tiled=True)
    gathered = arrived.reshape(EXPERTS * capacity, model_width)[slot_ids].astype(jnp.float32)
    gathered = gathered.reshape(per_block, TOPK, model_width)
    moe_sum = jnp.sum(gathered * route_gain[..., None], axis=1)
    return (resid + moe_sum).astype(jnp.bfloat16)


def solution(mesh):
    in_specs = (
        P("req", "head"),
        P("req", None),
        P("req", "head", None, None),
        P(),
        P(None, "head", None),
        P(None, "head", None),
        P("head", None, None),
        P(),
        P(("req", "head"), None),
        P(("req", "head"), None),
        P("req", None, None),
        P("req", None, None),
    )
    out_specs = P(("req", "head"), None)
    return jax.shard_map(local, mesh=mesh, in_specs=in_specs, out_specs=out_specs, check_vma=False)
```

```python
import math

import jax
import jax.numpy as jnp
from jax import lax
from jax.experimental import pallas as pl
from jax.experimental.pallas import tpu as pltpu
from jax.sharding import PartitionSpec as P

EXPERTS = 32
TOPK = 8
RATIO = 15
WIN = 512
TQ = 256
TK = 1536


floor_score = -1e30


def norm_rows(value_rows, gain_row):
    mean_square = jnp.mean(value_rows * value_rows, axis=-1, keepdims=True)
    return value_rows * lax.rsqrt(mean_square + 1e-05) * gain_row


def rope_tables(position, head_size):
    half_size = head_size // 2
    inverse = jnp.exp(
        jnp.arange(half_size, dtype=jnp.float32) * (-2.0 * math.log(10000.0) / head_size)
    )
    angles = position.astype(jnp.float32)[:, None] * inverse[None, :]
    angles = jnp.concatenate([angles, angles], axis=1)
    return (jnp.cos(angles), jnp.sin(angles))


def rotate(vectors, cos_part, sin_part):
    half_size = vectors.shape[-1] // 2
    turned = jnp.concatenate([-vectors[..., half_size:], vectors[..., :half_size]], axis=-1)
    return vectors * cos_part + turned * sin_part


def request_layout(counts, token_count, cache_ratio):
    end_rows = jnp.cumsum(counts)
    starts = end_rows - counts
    row_ids = jnp.arange(token_count, dtype=jnp.int32)
    segment = jnp.sum((row_ids[:, None] >= end_rows[None, :]).astype(jnp.int32), axis=1)
    member = (segment[:, None] == jnp.arange(counts.shape[0], dtype=jnp.int32)[None, :]).astype(
        jnp.int32
    )
    row_begin = jnp.sum(member * starts[None, :], axis=1)
    own_count = jnp.sum(member * counts[None, :], axis=1)
    position = cache_ratio * own_count + row_ids - row_begin
    return (starts, position)


def project(normed, query_weight, key_value_weight, position):
    token_count, model_width = normed.shape
    kv_heads = key_value_weight.shape[1]
    head_size = key_value_weight.shape[2] // 2
    group_size = query_weight.shape[2] // head_size
    query = jnp.dot(
        normed, query_weight.reshape(model_width, -1), preferred_element_type=jnp.float32
    )
    query = query.reshape(token_count, kv_heads, group_size, head_size)
    keyval = jnp.dot(
        normed, key_value_weight.reshape(model_width, -1), preferred_element_type=jnp.float32
    )
    keyval = keyval.reshape(token_count, kv_heads, 2 * head_size)
    cos_part, sin_part = rope_tables(position, head_size)
    query = rotate(query, cos_part[:, None, None, :], sin_part[:, None, None, :])
    query = (query * (1.0 / math.sqrt(head_size))).astype(jnp.bfloat16)
    new_key = rotate(keyval[..., :head_size], cos_part[:, None, :], sin_part[:, None, :]).astype(
        jnp.bfloat16
    )
    new_value = keyval[..., head_size:].astype(jnp.bfloat16)
    return (query, new_key, new_value)


def attn_kernel(counts_ref, q_ref, kv_ref, nkv_ref, o_ref, m_sc, l_sc, acc_sc):
    j = pl.program_id(0)
    qi = pl.program_id(1)
    kb = pl.program_id(2)
    last = pl.num_programs(2) - 1
    count = counts_ref[j]
    cached = RATIO * count
    groups, tq, width = q_ref.shape[1], q_ref.shape[2], q_ref.shape[3]
    tk = kv_ref.shape[2]
    win = nkv_ref.shape[1]
    tile_ok = qi * tq < count

    @pl.when(kb == 0)
    def _():
        m_sc[...] = jnp.full(m_sc.shape, floor_score, jnp.float32)
        l_sc[...] = jnp.zeros(l_sc.shape, jnp.float32)
        acc_sc[...] = jnp.zeros(acc_sc.shape, jnp.float32)

    def absorb(rows, mask):
        q = q_ref[0].reshape(groups * tq, width)
        s = lax.dot_general(
            q, rows, (((1,), (1,)), ((), ())), preferred_element_type=jnp.float32
        )
        s = s.reshape(groups, tq, rows.shape[0])
        if mask is not None:
            s = jnp.where(mask, s, floor_score)
        m_old = m_sc[...]
        m_new = jnp.maximum(m_old, jnp.max(s, axis=-1, keepdims=True))
        alpha = jnp.exp(m_old - m_new)
        p = jnp.exp(s - m_new)
        l_sc[...] = l_sc[...] * alpha + jnp.sum(p, axis=-1, keepdims=True)
        pv = jnp.dot(
            p.astype(jnp.bfloat16).reshape(groups * tq, rows.shape[0]),
            rows,
            preferred_element_type=jnp.float32,
        )
        acc_sc[...] = acc_sc[...] * alpha + pv.reshape(groups, tq, width)
        m_sc[...] = m_new

    @pl.when(tile_ok & (kb == 0))
    def _():
        row = qi * tq + lax.broadcasted_iota(jnp.int32, (1, tq, win), 1)
        col = lax.broadcasted_iota(jnp.int32, (1, tq, win), 2)
        absorb(nkv_ref[0], col <= row)

    @pl.when(tile_ok & (kb > 0) & ((kb - 1) * tk < cached))
    def _():
        col = (kb - 1) * tk + lax.broadcasted_iota(jnp.int32, (1, 1, tk), 2)
        absorb(kv_ref[0, 0], col < cached)

    @pl.when(kb == last)
    def _():
        total = l_sc[...]
        total = jnp.where(total > 0.0, total, 1.0)
        o_ref[0] = (acc_sc[...] / total).astype(o_ref.dtype)


def attention(counts, q_win, kv_cache, nkv_win):
    req_n, groups, win, width = q_win.shape
    cache_len = kv_cache.shape[2]
    n_tiles = win // TQ
    n_blocks = cache_len // TK

    def q_map(j, qi, kb, cnt):
        tiles = (cnt[j] + TQ - 1) // TQ
        return (j, 0, jnp.minimum(qi, tiles - 1), 0)

    def kv_map(j, qi, kb, cnt):
        tiles = (cnt[j] + TQ - 1) // TQ
        blocks = (RATIO * cnt[j] + TK - 1) // TK
        inner = jnp.clip(kb - 1, 0, blocks - 1)
        return (j, 0, jnp.where(qi < tiles, inner, blocks - 1), 0)

    grid_spec = pltpu.PrefetchScalarGridSpec(
        num_scalar_prefetch=1,
        grid=(req_n, n_tiles, n_blocks + 1),
        in_specs=[
            pl.BlockSpec((1, groups, TQ, width), q_map),
            pl.BlockSpec((1, 1, TK, width), kv_map),
            pl.BlockSpec((1, win, width), lambda j, qi, kb, cnt: (j, 0, 0)),
        ],
        out_specs=pl.BlockSpec((1, groups, TQ, width), lambda j, qi, kb, cnt: (j, 0, qi, 0)),
        scratch_shapes=[
            pltpu.VMEM((groups, TQ, 1), jnp.float32),
            pltpu.VMEM((groups, TQ, 1), jnp.float32),
            pltpu.VMEM((groups, TQ, width), jnp.float32),
        ],
    )
    return pl.pallas_call(
        attn_kernel,
        grid_spec=grid_spec,
        out_shape=jax.ShapeDtypeStruct(q_win.shape, jnp.bfloat16),
        compiler_params=pltpu.CompilerParams(
            dimension_semantics=("arbitrary", "arbitrary", "arbitrary")
        ),
    )(counts, q_win, kv_cache, nkv_win)


def local(
    tokens,
    new_counts,
    kv_cache,
    norm_attn,
    query_weight,
    key_value_weight,
    output_weight,
    norm_moe,
    routes,
    route_gain,
    w_gate_up,
    w_down,
):
    whole = lax.all_gather(tokens, "head", axis=1, tiled=True)
    token_count, model_width = whole.shape
    normed = norm_rows(whole.astype(jnp.float32), norm_attn).astype(jnp.bfloat16)
    counts = new_counts[0]
    starts, position = request_layout(counts, token_count, RATIO)
    query, new_key, new_value = project(normed, query_weight, key_value_weight, position)
    groups, head_size = query.shape[2], query.shape[3]
    req_n = counts.shape[0]
    width = 2 * head_size

    query = query.reshape(token_count, groups, head_size)
    query = jnp.concatenate([query, jnp.zeros_like(query)], axis=-1)
    query = jnp.concatenate([query, jnp.zeros((WIN,) + query.shape[1:], query.dtype)], axis=0)
    newkv = jnp.concatenate([new_key[:, 0], new_value[:, 0]], axis=-1)
    newkv = jnp.concatenate([newkv, jnp.zeros((WIN, width), newkv.dtype)], axis=0)
    q_win = jnp.stack(
        [lax.dynamic_slice_in_dim(query, starts[j], WIN, 0) for j in range(req_n)]
    )
    q_win = jnp.transpose(q_win, (0, 2, 1, 3))
    nkv_win = jnp.stack(
        [lax.dynamic_slice_in_dim(newkv, starts[j], WIN, 0) for j in range(req_n)]
    )
    out_win = attention(counts, q_win, kv_cache, nkv_win)
    out_win = jnp.transpose(out_win[..., head_size:], (0, 2, 1, 3)).reshape(
        req_n, WIN, groups * head_size
    )
    result = jnp.zeros((token_count + WIN, groups * head_size), jnp.bfloat16)
    for j in range(req_n):
        result = lax.dynamic_update_slice_in_dim(result, out_win[j], starts[j], 0)
    attn_out = result[:token_count]

    partial_value = jnp.dot(
        attn_out, output_weight.reshape(-1, model_width), preferred_element_type=jnp.float32
    )
    per_block = routes.shape[0]
    row_start = lax.axis_index("head") * per_block
    attn_rows = lax.psum_scatter(
        partial_value.astype(jnp.bfloat16), "head", scatter_dimension=0, tiled=True
    ).astype(jnp.float32)
    base_rows = lax.dynamic_slice_in_dim(whole, row_start, per_block, 0)
    resid = base_rows.astype(jnp.float32) + attn_rows
    moe_in = norm_rows(resid, norm_moe).astype(jnp.bfloat16)
    capacity = per_block // 2
    expert_ids = jnp.arange(EXPERTS, dtype=jnp.int32)
    onehot = (routes.reshape(-1)[:, None] == expert_ids[None, :]).astype(jnp.bfloat16)
    pair_count = onehot.shape[0]
    chunk = 32
    lower = (
        jnp.arange(chunk, dtype=jnp.int32)[:, None] > jnp.arange(chunk, dtype=jnp.int32)[None, :]
    ).astype(jnp.bfloat16)
    pieces = onehot.reshape(pair_count // chunk, chunk, EXPERTS)
    within = jnp.einsum("ij,cje->cie", lower, pieces, preferred_element_type=jnp.float32)
    piece_total = jnp.sum(pieces.astype(jnp.float32), axis=1)
    piece_lower = (
        jnp.arange(pair_count // chunk, dtype=jnp.int32)[:, None]
        > jnp.arange(pair_count // chunk, dtype=jnp.int32)[None, :]
    ).astype(jnp.float32)
    earlier = jnp.dot(piece_lower, piece_total, precision=lax.Precision.HIGHEST)
    before = (within + earlier[:, None, :]).reshape(pair_count, EXPERTS)
    rank_in = jnp.sum(before * onehot.astype(jnp.float32), axis=1).astype(jnp.int32)
    slot_ids = (routes.reshape(-1) * capacity + rank_in).reshape(per_block, TOPK)
    slot_range = jnp.arange(EXPERTS * capacity, dtype=jnp.int32)
    hits = slot_ids[:, :, None] == slot_range[None, None, :]
    send = jnp.any(hits, axis=1).astype(jnp.bfloat16)
    combine = jnp.sum(jnp.where(hits, route_gain[:, :, None], 0.0), axis=1)
    combine_hi = combine.astype(jnp.bfloat16)
    combine_lo = (combine - combine_hi.astype(jnp.float32)).astype(jnp.bfloat16)
    req_count = lax.axis_size("req")
    per_req = w_down.shape[0]
    ff_width = w_down.shape[1]
    outgoing = lax.dot_general(
        send, moe_in, (((0,), (0,)), ((), ())), preferred_element_type=jnp.float32
    ).astype(jnp.bfloat16)
    outgoing = outgoing.reshape(req_count, per_req, capacity, model_width)
    gate_up = jnp.einsum(
        "sncd,ndf->sncf",
        lax.all_to_all(outgoing, "req", split_axis=0, concat_axis=0, tiled=True),
        w_gate_up,
        preferred_element_type=jnp.float32,
    )
    hidden = (jax.nn.silu(gate_up[..., :ff_width]) * gate_up[..., ff_width:]).astype(jnp.bfloat16)
    produced = jnp.einsum(
        "sncf,nfd->sncd", hidden, w_down, preferred_element_type=jnp.float32
    ).astype(jnp.bfloat16)
    arrived = lax.all_to_all(produced, "req", split_axis=0, concat_axis=0, tiled=True)
    arrived = arrived.reshape(EXPERTS * capacity, model_width)
    moe_sum = jnp.dot(combine_hi, arrived, preferred_element_type=jnp.float32) + jnp.dot(
        combine_lo, arrived, preferred_element_type=jnp.float32
    )
    return (resid + moe_sum).astype(jnp.bfloat16)


def solution(mesh):
    in_specs = (
        P("req", "head"),
        P("req", None),
        P("req", "head", None, None),
        P(),
        P(None, "head", None),
        P(None, "head", None),
        P("head", None, None),
        P(),
        P(("req", "head"), None),
        P(("req", "head"), None),
        P("req", None, None),
        P("req", None, None),
    )
    out_specs = P(("req", "head"), None)
    return jax.shard_map(local, mesh=mesh, in_specs=in_specs, out_specs=out_specs, check_vma=False)
```

```python
import math

import jax
import jax.numpy as jnp
from jax import lax
from jax.experimental import pallas as pl
from jax.experimental.pallas import tpu as pltpu
from jax.sharding import PartitionSpec as P

EXPERTS = 32
TOPK = 8
RATIO = 15
WIN = 512
TQ = 256
TK = 1536


floor_score = -1e30


def norm_rows(value_rows, gain_row):
    mean_square = jnp.mean(value_rows * value_rows, axis=-1, keepdims=True)
    return value_rows * lax.rsqrt(mean_square + 1e-05) * gain_row


def rope_tables(position, head_size):
    half_size = head_size // 2
    inverse = jnp.exp(
        jnp.arange(half_size, dtype=jnp.float32) * (-2.0 * math.log(10000.0) / head_size)
    )
    angles = position.astype(jnp.float32)[:, None] * inverse[None, :]
    angles = jnp.concatenate([angles, angles], axis=1)
    return (jnp.cos(angles), jnp.sin(angles))


def rotate(vectors, cos_part, sin_part):
    half_size = vectors.shape[-1] // 2
    turned = jnp.concatenate([-vectors[..., half_size:], vectors[..., :half_size]], axis=-1)
    return vectors * cos_part + turned * sin_part


def request_layout(counts, token_count, cache_ratio):
    end_rows = jnp.cumsum(counts)
    starts = end_rows - counts
    row_ids = jnp.arange(token_count, dtype=jnp.int32)
    segment = jnp.sum((row_ids[:, None] >= end_rows[None, :]).astype(jnp.int32), axis=1)
    member = (segment[:, None] == jnp.arange(counts.shape[0], dtype=jnp.int32)[None, :]).astype(
        jnp.int32
    )
    row_begin = jnp.sum(member * starts[None, :], axis=1)
    own_count = jnp.sum(member * counts[None, :], axis=1)
    position = cache_ratio * own_count + row_ids - row_begin
    return (starts, position)


def project(normed, query_weight, key_value_weight, position):
    token_count, model_width = normed.shape
    kv_heads = key_value_weight.shape[1]
    head_size = key_value_weight.shape[2] // 2
    group_size = query_weight.shape[2] // head_size
    query = jnp.dot(
        normed, query_weight.reshape(model_width, -1), preferred_element_type=jnp.float32
    )
    query = query.reshape(token_count, kv_heads, group_size, head_size)
    keyval = jnp.dot(
        normed, key_value_weight.reshape(model_width, -1), preferred_element_type=jnp.float32
    )
    keyval = keyval.reshape(token_count, kv_heads, 2 * head_size)
    cos_part, sin_part = rope_tables(position, head_size)
    query = rotate(query, cos_part[:, None, None, :], sin_part[:, None, None, :])
    query = (query * (1.0 / math.sqrt(head_size))).astype(jnp.bfloat16)
    new_key = rotate(keyval[..., :head_size], cos_part[:, None, :], sin_part[:, None, :]).astype(
        jnp.bfloat16
    )
    new_value = keyval[..., head_size:].astype(jnp.bfloat16)
    return (query, new_key, new_value)


def attn_kernel(counts_ref, q_ref, kv_ref, nkv_ref, o_ref, m_sc, l_sc, acc_sc):
    j = pl.program_id(0)
    qi = pl.program_id(1)
    kb = pl.program_id(2)
    last = pl.num_programs(2) - 1
    count = counts_ref[j]
    cached = RATIO * count
    groups, tq, width = q_ref.shape[0], q_ref.shape[2], q_ref.shape[3]
    tk = kv_ref.shape[2]
    win = nkv_ref.shape[1]
    tile_ok = qi * tq < count

    @pl.when(kb == 0)
    def _():
        m_sc[...] = jnp.full(m_sc.shape, floor_score, jnp.float32)
        l_sc[...] = jnp.zeros(l_sc.shape, jnp.float32)
        acc_sc[...] = jnp.zeros(acc_sc.shape, jnp.float32)

    def absorb(rows, mask):
        q = q_ref[:, 0].reshape(groups * tq, width)
        s = lax.dot_general(
            q, rows, (((1,), (1,)), ((), ())), preferred_element_type=jnp.float32
        )
        s = s.reshape(groups, tq, rows.shape[0])
        if mask is not None:
            s = jnp.where(mask, s, floor_score)
        m_old = m_sc[...]
        m_new = jnp.maximum(m_old, jnp.max(s, axis=-1, keepdims=True))
        alpha = jnp.exp(m_old - m_new)
        p = jnp.exp(s - m_new)
        l_sc[...] = l_sc[...] * alpha + jnp.sum(p, axis=-1, keepdims=True)
        pv = jnp.dot(
            p.astype(jnp.bfloat16).reshape(groups * tq, rows.shape[0]),
            rows,
            preferred_element_type=jnp.float32,
        )
        acc_sc[...] = acc_sc[...] * alpha + pv.reshape(groups, tq, width)
        m_sc[...] = m_new

    @pl.when(tile_ok & (kb == 0))
    def _():
        row = qi * tq + lax.broadcasted_iota(jnp.int32, (1, tq, win), 1)
        col = lax.broadcasted_iota(jnp.int32, (1, tq, win), 2)
        absorb(nkv_ref[0], col <= row)

    @pl.when(tile_ok & (kb > 0) & ((kb - 1) * tk < cached))
    def _():
        col = (kb - 1) * tk + lax.broadcasted_iota(jnp.int32, (1, 1, tk), 2)
        absorb(kv_ref[0, 0], col < cached)

    @pl.when(kb == last)
    def _():
        total = l_sc[...]
        total = jnp.where(total > 0.0, total, 1.0)
        o_ref[:, 0] = (acc_sc[...] / total).astype(o_ref.dtype)


def attention(counts, q_win, kv_cache, nkv_win):
    groups, req_n, win, width = q_win.shape
    cache_len = kv_cache.shape[2]
    n_tiles = win // TQ
    n_blocks = cache_len // TK

    def q_map(j, qi, kb, cnt):
        tiles = (cnt[j] + TQ - 1) // TQ
        return (0, j, jnp.minimum(qi, tiles - 1), 0)

    def kv_map(j, qi, kb, cnt):
        tiles = (cnt[j] + TQ - 1) // TQ
        blocks = (RATIO * cnt[j] + TK - 1) // TK
        inner = jnp.clip(kb - 1, 0, blocks - 1)
        return (j, 0, jnp.where(qi < tiles, inner, blocks - 1), 0)

    grid_spec = pltpu.PrefetchScalarGridSpec(
        num_scalar_prefetch=1,
        grid=(req_n, n_tiles, n_blocks + 1),
        in_specs=[
            pl.BlockSpec((groups, 1, TQ, width), q_map),
            pl.BlockSpec((1, 1, TK, width), kv_map),
            pl.BlockSpec((1, win, width), lambda j, qi, kb, cnt: (j, 0, 0)),
        ],
        out_specs=pl.BlockSpec((groups, 1, TQ, width), lambda j, qi, kb, cnt: (0, j, qi, 0)),
        scratch_shapes=[
            pltpu.VMEM((groups, TQ, 1), jnp.float32),
            pltpu.VMEM((groups, TQ, 1), jnp.float32),
            pltpu.VMEM((groups, TQ, width), jnp.float32),
        ],
    )
    return pl.pallas_call(
        attn_kernel,
        grid_spec=grid_spec,
        out_shape=jax.ShapeDtypeStruct(q_win.shape, jnp.bfloat16),
        compiler_params=pltpu.CompilerParams(
            dimension_semantics=("arbitrary", "arbitrary", "arbitrary")
        ),
    )(counts, q_win, kv_cache, nkv_win)


def turned_columns(weight):
    half = weight.shape[-1] // 2
    return jnp.concatenate([-weight[..., half:], weight[..., :half]], axis=-1)


def local(
    tokens,
    new_counts,
    kv_cache,
    norm_attn,
    query_weight,
    key_value_weight,
    output_weight,
    norm_moe,
    routes,
    route_gain,
    w_gate_up,
    w_down,
):
    whole = lax.all_gather(tokens, "head", axis=1, tiled=True)
    token_count, model_width = whole.shape
    normed = norm_rows(whole.astype(jnp.float32), norm_attn).astype(jnp.bfloat16)
    counts = new_counts[0]
    starts, position = request_layout(counts, token_count, RATIO)
    req_n = counts.shape[0]
    head_size = key_value_weight.shape[2] // 2
    groups = query_weight.shape[2] // head_size
    width = 2 * head_size

    cos_part, sin_part = rope_tables(position, head_size)
    scale = 1.0 / math.sqrt(head_size)
    no_lanes = jnp.zeros((token_count, width - head_size), jnp.float32)
    cos_q = jnp.concatenate([cos_part * scale, no_lanes], axis=1)
    sin_q = jnp.concatenate([sin_part * scale, no_lanes], axis=1)
    q_weight = query_weight.reshape(model_width, groups, head_size)
    no_cols = jnp.zeros((model_width, groups, width - head_size), q_weight.dtype)
    q_plain = jnp.concatenate([q_weight, no_cols], axis=-1)
    q_turned = jnp.concatenate([turned_columns(q_weight), no_cols], axis=-1)
    q_a = jnp.einsum("td,dgc->gtc", normed, q_plain, preferred_element_type=jnp.float32)
    q_b = jnp.einsum("td,dgc->gtc", normed, q_turned, preferred_element_type=jnp.float32)
    query = (q_a * cos_q[None] + q_b * sin_q[None]).astype(jnp.bfloat16)

    kv_weight = key_value_weight.reshape(model_width, width)
    k_turned = jnp.concatenate(
        [turned_columns(kv_weight[:, :head_size]), jnp.zeros_like(kv_weight[:, head_size:])],
        axis=1,
    )
    ones_lanes = jnp.ones((token_count, width - head_size), jnp.float32)
    cos_k = jnp.concatenate([cos_part, ones_lanes], axis=1)
    sin_k = jnp.concatenate([sin_part, no_lanes], axis=1)
    kv_a = jnp.dot(normed, kv_weight, preferred_element_type=jnp.float32)
    kv_b = jnp.dot(normed, k_turned, preferred_element_type=jnp.float32)
    newkv = (kv_a * cos_k + kv_b * sin_k).astype(jnp.bfloat16)

    row_ids = jnp.arange(token_count, dtype=jnp.int32)
    offsets = jnp.arange(WIN, dtype=jnp.int32)
    select = (row_ids[:, None, None] == starts[None, :, None] + offsets[None, None, :]) & (
        offsets[None, None, :] < counts[None, :, None]
    )
    select = select.astype(jnp.bfloat16).reshape(token_count, req_n * WIN)
    q_win = jnp.einsum("tw,gtc->gwc", select, query, preferred_element_type=jnp.float32)
    q_win = q_win.astype(jnp.bfloat16).reshape(groups, req_n, WIN, width)
    nkv_win = jnp.einsum("tw,tc->wc", select, newkv, preferred_element_type=jnp.float32)
    nkv_win = nkv_win.astype(jnp.bfloat16).reshape(req_n, WIN, width)
    out_win = attention(counts, q_win, kv_cache, nkv_win)
    out_win = out_win.reshape(groups, req_n * WIN, width)
    attn_rows = jnp.einsum("tw,gwc->gtc", select, out_win, preferred_element_type=jnp.float32)
    attn_rows = attn_rows.astype(jnp.bfloat16)
    o_weight = output_weight.reshape(groups, head_size, model_width)
    o_weight = jnp.concatenate([jnp.zeros_like(o_weight), o_weight], axis=1)

    partial_value = jnp.einsum(
        "gtc,gcd->td", attn_rows, o_weight, preferred_element_type=jnp.float32
    )
    per_block = routes.shape[0]
    row_start = lax.axis_index("head") * per_block
    summed = lax.psum_scatter(
        partial_value.astype(jnp.bfloat16), "head", scatter_dimension=0, tiled=True
    ).astype(jnp.float32)
    base_rows = lax.dynamic_slice_in_dim(whole, row_start, per_block, 0)
    resid = base_rows.astype(jnp.float32) + summed
    moe_in = norm_rows(resid, norm_moe).astype(jnp.bfloat16)
    capacity = per_block // 2
    expert_ids = jnp.arange(EXPERTS, dtype=jnp.int32)
    onehot = (routes.reshape(-1)[:, None] == expert_ids[None, :]).astype(jnp.bfloat16)
    pair_count = onehot.shape[0]
    chunk = 32
    lower = (
        jnp.arange(chunk, dtype=jnp.int32)[:, None] > jnp.arange(chunk, dtype=jnp.int32)[None, :]
    ).astype(jnp.bfloat16)
    pieces = onehot.reshape(pair_count // chunk, chunk, EXPERTS)
    within = jnp.einsum("ij,cje->cie", lower, pieces, preferred_element_type=jnp.float32)
    piece_total = jnp.sum(pieces.astype(jnp.float32), axis=1)
    piece_lower = (
        jnp.arange(pair_count // chunk, dtype=jnp.int32)[:, None]
        > jnp.arange(pair_count // chunk, dtype=jnp.int32)[None, :]
    ).astype(jnp.float32)
    earlier = jnp.dot(piece_lower, piece_total, precision=lax.Precision.HIGHEST)
    before = (within + earlier[:, None, :]).reshape(pair_count, EXPERTS)
    rank_in = jnp.sum(before * onehot.astype(jnp.float32), axis=1).astype(jnp.int32)
    slot_ids = (routes.reshape(-1) * capacity + rank_in).reshape(per_block, TOPK)
    slot_range = jnp.arange(EXPERTS * capacity, dtype=jnp.int32)
    hits = slot_ids[:, :, None] == slot_range[None, None, :]
    send = jnp.any(hits, axis=1).astype(jnp.bfloat16)
    combine = jnp.sum(jnp.where(hits, route_gain[:, :, None], 0.0), axis=1)
    combine_hi = combine.astype(jnp.bfloat16)
    combine_lo = (combine - combine_hi.astype(jnp.float32)).astype(jnp.bfloat16)
    req_count = lax.axis_size("req")
    per_req = w_down.shape[0]
    ff_width = w_down.shape[1]
    outgoing = lax.dot_general(
        send, moe_in, (((0,), (0,)), ((), ())), preferred_element_type=jnp.float32
    ).astype(jnp.bfloat16)
    outgoing = outgoing.reshape(req_count, per_req, capacity, model_width)
    gate_up = jnp.einsum(
        "sncd,ndf->sncf",
        lax.all_to_all(outgoing, "req", split_axis=0, concat_axis=0, tiled=True),
        w_gate_up,
        preferred_element_type=jnp.float32,
    )
    hidden = (jax.nn.silu(gate_up[..., :ff_width]) * gate_up[..., ff_width:]).astype(jnp.bfloat16)
    produced = jnp.einsum(
        "sncf,nfd->sncd", hidden, w_down, preferred_element_type=jnp.float32
    ).astype(jnp.bfloat16)
    arrived = lax.all_to_all(produced, "req", split_axis=0, concat_axis=0, tiled=True)
    arrived = arrived.reshape(EXPERTS * capacity, model_width)
    moe_sum = jnp.dot(combine_hi, arrived, preferred_element_type=jnp.float32) + jnp.dot(
        combine_lo, arrived, preferred_element_type=jnp.float32
    )
    return (resid + moe_sum).astype(jnp.bfloat16)


def solution(mesh):
    in_specs = (
        P("req", "head"),
        P("req", None),
        P("req", "head", None, None),
        P(),
        P(None, "head", None),
        P(None, "head", None),
        P("head", None, None),
        P(),
        P(("req", "head"), None),
        P(("req", "head"), None),
        P("req", None, None),
        P("req", None, None),
    )
    out_specs = P(("req", "head"), None)
    return jax.shard_map(local, mesh=mesh, in_specs=in_specs, out_specs=out_specs, check_vma=False)
```

```python
import math

import jax
import jax.numpy as jnp
from jax import lax
from jax.experimental import pallas as pl
from jax.experimental.pallas import tpu as pltpu
from jax.sharding import PartitionSpec as P

EXPERTS = 32
TOPK = 8
RATIO = 15
WIN = 512
TQ = 256
TK = 1536


floor_score = -1e30


def norm_rows(value_rows, gain_row):
    mean_square = jnp.mean(value_rows * value_rows, axis=-1, keepdims=True)
    return value_rows * lax.rsqrt(mean_square + 1e-05) * gain_row


def rope_tables(position, head_size):
    half_size = head_size // 2
    inverse = jnp.exp(
        jnp.arange(half_size, dtype=jnp.float32) * (-2.0 * math.log(10000.0) / head_size)
    )
    angles = position.astype(jnp.float32)[:, None] * inverse[None, :]
    angles = jnp.concatenate([angles, angles], axis=1)
    return (jnp.cos(angles), jnp.sin(angles))


def rotate(vectors, cos_part, sin_part):
    half_size = vectors.shape[-1] // 2
    turned = jnp.concatenate([-vectors[..., half_size:], vectors[..., :half_size]], axis=-1)
    return vectors * cos_part + turned * sin_part


def request_layout(counts, token_count, cache_ratio):
    end_rows = jnp.cumsum(counts)
    starts = end_rows - counts
    row_ids = jnp.arange(token_count, dtype=jnp.int32)
    segment = jnp.sum((row_ids[:, None] >= end_rows[None, :]).astype(jnp.int32), axis=1)
    member = (segment[:, None] == jnp.arange(counts.shape[0], dtype=jnp.int32)[None, :]).astype(
        jnp.int32
    )
    row_begin = jnp.sum(member * starts[None, :], axis=1)
    own_count = jnp.sum(member * counts[None, :], axis=1)
    position = cache_ratio * own_count + row_ids - row_begin
    return (starts, position)


def project(normed, query_weight, key_value_weight, position):
    token_count, model_width = normed.shape
    kv_heads = key_value_weight.shape[1]
    head_size = key_value_weight.shape[2] // 2
    group_size = query_weight.shape[2] // head_size
    query = jnp.dot(
        normed, query_weight.reshape(model_width, -1), preferred_element_type=jnp.float32
    )
    query = query.reshape(token_count, kv_heads, group_size, head_size)
    keyval = jnp.dot(
        normed, key_value_weight.reshape(model_width, -1), preferred_element_type=jnp.float32
    )
    keyval = keyval.reshape(token_count, kv_heads, 2 * head_size)
    cos_part, sin_part = rope_tables(position, head_size)
    query = rotate(query, cos_part[:, None, None, :], sin_part[:, None, None, :])
    query = (query * (1.0 / math.sqrt(head_size))).astype(jnp.bfloat16)
    new_key = rotate(keyval[..., :head_size], cos_part[:, None, :], sin_part[:, None, :]).astype(
        jnp.bfloat16
    )
    new_value = keyval[..., head_size:].astype(jnp.bfloat16)
    return (query, new_key, new_value)


def attn_kernel(counts_ref, q_ref, kv_ref, nkv_ref, o_ref, m_sc, l_sc, acc_sc):
    j = pl.program_id(0)
    qi = pl.program_id(1)
    kb = pl.program_id(2)
    last = pl.num_programs(2) - 1
    count = counts_ref[j]
    cached = RATIO * count
    groups, tq, width = q_ref.shape[0], q_ref.shape[2], q_ref.shape[3]
    tk = kv_ref.shape[2]
    win = nkv_ref.shape[1]
    tile_ok = qi * tq < count

    @pl.when(kb == 0)
    def _():
        m_sc[...] = jnp.full(m_sc.shape, floor_score, jnp.float32)
        l_sc[...] = jnp.zeros(l_sc.shape, jnp.float32)
        acc_sc[...] = jnp.zeros(acc_sc.shape, jnp.float32)

    def absorb(rows, mask):
        q = q_ref[:, 0].reshape(groups * tq, width)
        s = lax.dot_general(
            q, rows, (((1,), (1,)), ((), ())), preferred_element_type=jnp.float32
        )
        s = s.reshape(groups, tq, rows.shape[0])
        if mask is not None:
            s = jnp.where(mask, s, floor_score)
        m_old = m_sc[...]
        m_new = jnp.maximum(m_old, jnp.max(s, axis=-1, keepdims=True))
        alpha = jnp.exp(m_old - m_new)
        p = jnp.exp(s - m_new)
        l_sc[...] = l_sc[...] * alpha + jnp.sum(p, axis=-1, keepdims=True)
        pv = jnp.dot(
            p.astype(jnp.bfloat16).reshape(groups * tq, rows.shape[0]),
            rows,
            preferred_element_type=jnp.float32,
        )
        acc_sc[...] = acc_sc[...] * alpha + pv.reshape(groups, tq, width)
        m_sc[...] = m_new

    @pl.when(tile_ok & (kb == 0))
    def _():
        row = qi * tq + lax.broadcasted_iota(jnp.int32, (1, tq, win), 1)
        col = lax.broadcasted_iota(jnp.int32, (1, tq, win), 2)
        absorb(nkv_ref[0], col <= row)

    @pl.when(tile_ok & (kb > 0) & ((kb - 1) * tk < cached))
    def _():
        col = (kb - 1) * tk + lax.broadcasted_iota(jnp.int32, (1, 1, tk), 2)
        absorb(kv_ref[0, 0], col < cached)

    @pl.when(kb == last)
    def _():
        total = l_sc[...]
        total = jnp.where(total > 0.0, total, 1.0)
        o_ref[:, 0] = (acc_sc[...] / total).astype(o_ref.dtype)


def attention(counts, q_win, kv_cache, nkv_win):
    groups, req_n, win, width = q_win.shape
    cache_len = kv_cache.shape[2]
    n_tiles = win // TQ
    n_blocks = cache_len // TK

    def q_map(j, qi, kb, cnt):
        tiles = (cnt[j] + TQ - 1) // TQ
        return (0, j, jnp.minimum(qi, tiles - 1), 0)

    def kv_map(j, qi, kb, cnt):
        tiles = (cnt[j] + TQ - 1) // TQ
        blocks = (RATIO * cnt[j] + TK - 1) // TK
        inner = jnp.clip(kb - 1, 0, blocks - 1)
        return (j, 0, jnp.where(qi < tiles, inner, blocks - 1), 0)

    grid_spec = pltpu.PrefetchScalarGridSpec(
        num_scalar_prefetch=1,
        grid=(req_n, n_tiles, n_blocks + 1),
        in_specs=[
            pl.BlockSpec((groups, 1, TQ, width), q_map),
            pl.BlockSpec((1, 1, TK, width), kv_map),
            pl.BlockSpec((1, win, width), lambda j, qi, kb, cnt: (j, 0, 0)),
        ],
        out_specs=pl.BlockSpec((groups, 1, TQ, width), lambda j, qi, kb, cnt: (0, j, qi, 0)),
        scratch_shapes=[
            pltpu.VMEM((groups, TQ, 1), jnp.float32),
            pltpu.VMEM((groups, TQ, 1), jnp.float32),
            pltpu.VMEM((groups, TQ, width), jnp.float32),
        ],
    )
    return pl.pallas_call(
        attn_kernel,
        grid_spec=grid_spec,
        out_shape=jax.ShapeDtypeStruct(q_win.shape, jnp.bfloat16),
        compiler_params=pltpu.CompilerParams(
            dimension_semantics=("arbitrary", "arbitrary", "arbitrary")
        ),
    )(counts, q_win, kv_cache, nkv_win)


def turned_columns(weight):
    half = weight.shape[-1] // 2
    return jnp.concatenate([-weight[..., half:], weight[..., :half]], axis=-1)


def local(
    tokens,
    new_counts,
    kv_cache,
    norm_attn,
    query_weight,
    key_value_weight,
    output_weight,
    norm_moe,
    routes,
    route_gain,
    w_gate_up,
    w_down,
):
    whole = lax.all_gather(tokens, "head", axis=1, tiled=True)
    o_weight_all = lax.all_gather(output_weight, "head", axis=0, tiled=True)
    token_count, model_width = whole.shape
    normed = norm_rows(whole.astype(jnp.float32), norm_attn).astype(jnp.bfloat16)
    counts = new_counts[0]
    starts, position = request_layout(counts, token_count, RATIO)
    req_n = counts.shape[0]
    head_size = key_value_weight.shape[2] // 2
    groups = query_weight.shape[2] // head_size
    width = 2 * head_size

    cos_part, sin_part = rope_tables(position, head_size)
    scale = 1.0 / math.sqrt(head_size)
    no_lanes = jnp.zeros((token_count, width - head_size), jnp.float32)
    cos_q = jnp.concatenate([cos_part * scale, no_lanes], axis=1)
    sin_q = jnp.concatenate([sin_part * scale, no_lanes], axis=1)
    q_weight = query_weight.reshape(model_width, groups, head_size)
    no_cols = jnp.zeros((model_width, groups, width - head_size), q_weight.dtype)
    q_plain = jnp.concatenate([q_weight, no_cols], axis=-1)
    q_turned = jnp.concatenate([turned_columns(q_weight), no_cols], axis=-1)
    q_a = jnp.einsum("td,dgc->gtc", normed, q_plain, preferred_element_type=jnp.float32)
    q_b = jnp.einsum("td,dgc->gtc", normed, q_turned, preferred_element_type=jnp.float32)
    query = (q_a * cos_q[None] + q_b * sin_q[None]).astype(jnp.bfloat16)

    kv_weight = key_value_weight.reshape(model_width, width)
    k_turned = jnp.concatenate(
        [turned_columns(kv_weight[:, :head_size]), jnp.zeros_like(kv_weight[:, head_size:])],
        axis=1,
    )
    ones_lanes = jnp.ones((token_count, width - head_size), jnp.float32)
    cos_k = jnp.concatenate([cos_part, ones_lanes], axis=1)
    sin_k = jnp.concatenate([sin_part, no_lanes], axis=1)
    kv_a = jnp.dot(normed, kv_weight, preferred_element_type=jnp.float32)
    kv_b = jnp.dot(normed, k_turned, preferred_element_type=jnp.float32)
    newkv = (kv_a * cos_k + kv_b * sin_k).astype(jnp.bfloat16)

    row_ids = jnp.arange(token_count, dtype=jnp.int32)
    offsets = jnp.arange(WIN, dtype=jnp.int32)
    select = (row_ids[:, None, None] == starts[None, :, None] + offsets[None, None, :]) & (
        offsets[None, None, :] < counts[None, :, None]
    )
    select = select.astype(jnp.bfloat16).reshape(token_count, req_n * WIN)
    q_win = jnp.einsum("tw,gtc->gwc", select, query, preferred_element_type=jnp.float32)
    q_win = q_win.astype(jnp.bfloat16).reshape(groups, req_n, WIN, width)
    nkv_win = jnp.einsum("tw,tc->wc", select, newkv, preferred_element_type=jnp.float32)
    nkv_win = nkv_win.astype(jnp.bfloat16).reshape(req_n, WIN, width)
    out_win = attention(counts, q_win, kv_cache, nkv_win)
    out_win = out_win[..., head_size:].reshape(groups, req_n * WIN, head_size)
    attn_rows = jnp.einsum("tw,gwc->gtc", select, out_win, preferred_element_type=jnp.float32)
    attn_rows = attn_rows.astype(jnp.bfloat16)
    n_head = lax.axis_size("head")
    per_block = routes.shape[0]
    row_start = lax.axis_index("head") * per_block
    leaving = jnp.transpose(attn_rows.reshape(groups, n_head, per_block, head_size), (1, 0, 2, 3))
    arriving = lax.all_to_all(leaving, "head", split_axis=0, concat_axis=0, tiled=True)
    o_weight = o_weight_all.reshape(n_head, groups, head_size, model_width)
    summed = jnp.einsum(
        "hgtc,hgcd->td", arriving, o_weight, preferred_element_type=jnp.float32
    )
    base_rows = lax.dynamic_slice_in_dim(whole, row_start, per_block, 0)
    resid = base_rows.astype(jnp.float32) + summed
    moe_in = norm_rows(resid, norm_moe).astype(jnp.bfloat16)
    capacity = per_block // 2
    expert_ids = jnp.arange(EXPERTS, dtype=jnp.int32)
    onehot = (routes.reshape(-1)[:, None] == expert_ids[None, :]).astype(jnp.bfloat16)
    pair_count = onehot.shape[0]
    chunk = 32
    lower = (
        jnp.arange(chunk, dtype=jnp.int32)[:, None] > jnp.arange(chunk, dtype=jnp.int32)[None, :]
    ).astype(jnp.bfloat16)
    pieces = onehot.reshape(pair_count // chunk, chunk, EXPERTS)
    within = jnp.einsum("ij,cje->cie", lower, pieces, preferred_element_type=jnp.float32)
    piece_total = jnp.sum(pieces.astype(jnp.float32), axis=1)
    piece_lower = (
        jnp.arange(pair_count // chunk, dtype=jnp.int32)[:, None]
        > jnp.arange(pair_count // chunk, dtype=jnp.int32)[None, :]
    ).astype(jnp.float32)
    earlier = jnp.dot(piece_lower, piece_total, precision=lax.Precision.HIGHEST)
    before = (within + earlier[:, None, :]).reshape(pair_count, EXPERTS)
    rank_in = jnp.sum(before * onehot.astype(jnp.float32), axis=1).astype(jnp.int32)
    slot_ids = (routes.reshape(-1) * capacity + rank_in).reshape(per_block, TOPK)
    slot_range = jnp.arange(EXPERTS * capacity, dtype=jnp.int32)
    hits = slot_ids[:, :, None] == slot_range[None, None, :]
    send = jnp.any(hits, axis=1).astype(jnp.bfloat16)
    combine = jnp.sum(jnp.where(hits, route_gain[:, :, None], 0.0), axis=1)
    combine_hi = combine.astype(jnp.bfloat16)
    combine_lo = (combine - combine_hi.astype(jnp.float32)).astype(jnp.bfloat16)
    req_count = lax.axis_size("req")
    per_req = w_down.shape[0]
    ff_width = w_down.shape[1]
    outgoing = lax.dot_general(
        send, moe_in, (((0,), (0,)), ((), ())), preferred_element_type=jnp.float32
    ).astype(jnp.bfloat16)
    outgoing = outgoing.reshape(req_count, per_req, capacity, model_width)
    gate_up = jnp.einsum(
        "sncd,ndf->sncf",
        lax.all_to_all(outgoing, "req", split_axis=0, concat_axis=0, tiled=True),
        w_gate_up,
        preferred_element_type=jnp.float32,
    )
    hidden = (jax.nn.silu(gate_up[..., :ff_width]) * gate_up[..., ff_width:]).astype(jnp.bfloat16)
    produced = jnp.einsum(
        "sncf,nfd->sncd", hidden, w_down, preferred_element_type=jnp.float32
    ).astype(jnp.bfloat16)
    arrived = lax.all_to_all(produced, "req", split_axis=0, concat_axis=0, tiled=True)
    arrived = arrived.reshape(EXPERTS * capacity, model_width)
    moe_sum = jnp.dot(combine_hi, arrived, preferred_element_type=jnp.float32) + jnp.dot(
        combine_lo, arrived, preferred_element_type=jnp.float32
    )
    return (resid + moe_sum).astype(jnp.bfloat16)


def solution(mesh):
    in_specs = (
        P("req", "head"),
        P("req", None),
        P("req", "head", None, None),
        P(),
        P(None, "head", None),
        P(None, "head", None),
        P("head", None, None),
        P(),
        P(("req", "head"), None),
        P(("req", "head"), None),
        P("req", None, None),
        P("req", None, None),
    )
    out_specs = P(("req", "head"), None)
    return jax.shard_map(local, mesh=mesh, in_specs=in_specs, out_specs=out_specs, check_vma=False)
```

```python
import math

import jax
import jax.numpy as jnp
from jax import lax
from jax.experimental import pallas as pl
from jax.experimental.pallas import tpu as pltpu
from jax.sharding import PartitionSpec as P

EXPERTS = 32
TOPK = 8
RATIO = 15
WIN = 512
TQ = 256
TK = 1536


floor_score = -1e30


def norm_rows(value_rows, gain_row):
    mean_square = jnp.mean(value_rows * value_rows, axis=-1, keepdims=True)
    return value_rows * lax.rsqrt(mean_square + 1e-05) * gain_row


def rope_tables(position, head_size):
    half_size = head_size // 2
    inverse = jnp.exp(
        jnp.arange(half_size, dtype=jnp.float32) * (-2.0 * math.log(10000.0) / head_size)
    )
    angles = position.astype(jnp.float32)[:, None] * inverse[None, :]
    angles = jnp.concatenate([angles, angles], axis=1)
    return (jnp.cos(angles), jnp.sin(angles))


def rotate(vectors, cos_part, sin_part):
    half_size = vectors.shape[-1] // 2
    turned = jnp.concatenate([-vectors[..., half_size:], vectors[..., :half_size]], axis=-1)
    return vectors * cos_part + turned * sin_part


def request_layout(counts, token_count, cache_ratio):
    end_rows = jnp.cumsum(counts)
    starts = end_rows - counts
    row_ids = jnp.arange(token_count, dtype=jnp.int32)
    segment = jnp.sum((row_ids[:, None] >= end_rows[None, :]).astype(jnp.int32), axis=1)
    member = (segment[:, None] == jnp.arange(counts.shape[0], dtype=jnp.int32)[None, :]).astype(
        jnp.int32
    )
    row_begin = jnp.sum(member * starts[None, :], axis=1)
    own_count = jnp.sum(member * counts[None, :], axis=1)
    position = cache_ratio * own_count + row_ids - row_begin
    return (starts, position)


def project(normed, query_weight, key_value_weight, position):
    token_count, model_width = normed.shape
    kv_heads = key_value_weight.shape[1]
    head_size = key_value_weight.shape[2] // 2
    group_size = query_weight.shape[2] // head_size
    query = jnp.dot(
        normed, query_weight.reshape(model_width, -1), preferred_element_type=jnp.float32
    )
    query = query.reshape(token_count, kv_heads, group_size, head_size)
    keyval = jnp.dot(
        normed, key_value_weight.reshape(model_width, -1), preferred_element_type=jnp.float32
    )
    keyval = keyval.reshape(token_count, kv_heads, 2 * head_size)
    cos_part, sin_part = rope_tables(position, head_size)
    query = rotate(query, cos_part[:, None, None, :], sin_part[:, None, None, :])
    query = (query * (1.0 / math.sqrt(head_size))).astype(jnp.bfloat16)
    new_key = rotate(keyval[..., :head_size], cos_part[:, None, :], sin_part[:, None, :]).astype(
        jnp.bfloat16
    )
    new_value = keyval[..., head_size:].astype(jnp.bfloat16)
    return (query, new_key, new_value)


def attn_kernel(counts_ref, q_ref, kv_ref, nkv_ref, o_ref, m_sc, l_sc, acc_sc):
    j = pl.program_id(0)
    qi = pl.program_id(1)
    kb = pl.program_id(2)
    last = pl.num_programs(2) - 1
    count = counts_ref[j]
    cached = RATIO * count
    groups, tq, width = q_ref.shape[0], q_ref.shape[2], q_ref.shape[3]
    tk = kv_ref.shape[2]
    win = nkv_ref.shape[1]
    tile_ok = qi * tq < count

    @pl.when(kb == 0)
    def _():
        m_sc[...] = jnp.full(m_sc.shape, floor_score, jnp.float32)
        l_sc[...] = jnp.zeros(l_sc.shape, jnp.float32)
        acc_sc[...] = jnp.zeros(acc_sc.shape, jnp.float32)

    def absorb_group(g, rows, mask):
        s = lax.dot_general(
            q_ref[g, 0], rows, (((1,), (1,)), ((), ())), preferred_element_type=jnp.float32
        )
        s = jnp.where(mask, s, floor_score)
        m_old = m_sc[g]
        m_new = jnp.maximum(m_old, jnp.max(s, axis=-1, keepdims=True))
        alpha = jnp.exp(m_old - m_new)
        p = jnp.exp(s - m_new)
        l_sc[g] = l_sc[g] * alpha + jnp.sum(p, axis=-1, keepdims=True)
        pv = jnp.dot(p.astype(jnp.bfloat16), rows, preferred_element_type=jnp.float32)
        acc_sc[g] = acc_sc[g] * alpha + pv
        m_sc[g] = m_new

    @pl.when(tile_ok & (kb == 0))
    def _():
        row = qi * tq + lax.broadcasted_iota(jnp.int32, (tq, win), 0)
        col = lax.broadcasted_iota(jnp.int32, (tq, win), 1)

        def one_group(g, carry):
            absorb_group(g, nkv_ref[0], col <= row)
            return carry

        lax.fori_loop(0, groups, one_group, 0)

    @pl.when(tile_ok & (kb > 0) & ((kb - 1) * tk < cached))
    def _():
        pieces = tk // win

        def one_piece(step, carry):
            g = step // pieces
            at = (step % pieces) * win
            col = (kb - 1) * tk + at + lax.broadcasted_iota(jnp.int32, (1, win), 1)
            absorb_group(g, kv_ref[0, 0, pl.ds(pl.multiple_of(at, win), win), :], col < cached)
            return carry

        lax.fori_loop(0, groups * pieces, one_piece, 0)

    @pl.when(kb == last)
    def _():
        total = l_sc[...]
        total = jnp.where(total > 0.0, total, 1.0)
        o_ref[:, 0] = (acc_sc[...] / total).astype(o_ref.dtype)


def attention(counts, q_win, kv_cache, nkv_win):
    groups, req_n, win, width = q_win.shape
    cache_len = kv_cache.shape[2]
    n_tiles = win // TQ
    n_blocks = cache_len // TK

    def q_map(j, qi, kb, cnt):
        tiles = (cnt[j] + TQ - 1) // TQ
        return (0, j, jnp.minimum(qi, tiles - 1), 0)

    def kv_map(j, qi, kb, cnt):
        tiles = (cnt[j] + TQ - 1) // TQ
        blocks = (RATIO * cnt[j] + TK - 1) // TK
        inner = jnp.clip(kb - 1, 0, blocks - 1)
        return (j, 0, jnp.where(qi < tiles, inner, blocks - 1), 0)

    grid_spec = pltpu.PrefetchScalarGridSpec(
        num_scalar_prefetch=1,
        grid=(req_n, n_tiles, n_blocks + 1),
        in_specs=[
            pl.BlockSpec((groups, 1, TQ, width), q_map),
            pl.BlockSpec((1, 1, TK, width), kv_map),
            pl.BlockSpec((1, win, width), lambda j, qi, kb, cnt: (j, 0, 0)),
        ],
        out_specs=pl.BlockSpec((groups, 1, TQ, width), lambda j, qi, kb, cnt: (0, j, qi, 0)),
        scratch_shapes=[
            pltpu.VMEM((groups, TQ, 1), jnp.float32),
            pltpu.VMEM((groups, TQ, 1), jnp.float32),
            pltpu.VMEM((groups, TQ, width), jnp.float32),
        ],
    )
    return pl.pallas_call(
        attn_kernel,
        grid_spec=grid_spec,
        out_shape=jax.ShapeDtypeStruct(q_win.shape, jnp.bfloat16),
        compiler_params=pltpu.CompilerParams(
            dimension_semantics=("arbitrary", "arbitrary", "arbitrary")
        ),
    )(counts, q_win, kv_cache, nkv_win)


def turned_columns(weight):
    half = weight.shape[-1] // 2
    return jnp.concatenate([-weight[..., half:], weight[..., :half]], axis=-1)


def local(
    tokens,
    new_counts,
    kv_cache,
    norm_attn,
    query_weight,
    key_value_weight,
    output_weight,
    norm_moe,
    routes,
    route_gain,
    w_gate_up,
    w_down,
):
    whole = lax.all_gather(tokens, "head", axis=1, tiled=True)
    o_weight_all = lax.all_gather(output_weight, "head", axis=0, tiled=True)
    token_count, model_width = whole.shape
    normed = norm_rows(whole.astype(jnp.float32), norm_attn).astype(jnp.bfloat16)
    counts = new_counts[0]
    starts, position = request_layout(counts, token_count, RATIO)
    req_n = counts.shape[0]
    head_size = key_value_weight.shape[2] // 2
    groups = query_weight.shape[2] // head_size
    width = 2 * head_size

    cos_part, sin_part = rope_tables(position, head_size)
    scale = 1.0 / math.sqrt(head_size)
    no_lanes = jnp.zeros((token_count, width - head_size), jnp.float32)
    cos_q = jnp.concatenate([cos_part * scale, no_lanes], axis=1)
    sin_q = jnp.concatenate([sin_part * scale, no_lanes], axis=1)
    q_weight = query_weight.reshape(model_width, groups, head_size)
    no_cols = jnp.zeros((model_width, groups, width - head_size), q_weight.dtype)
    q_plain = jnp.concatenate([q_weight, no_cols], axis=-1)
    q_turned = jnp.concatenate([turned_columns(q_weight), no_cols], axis=-1)
    q_a = jnp.einsum("td,dgc->gtc", normed, q_plain, preferred_element_type=jnp.float32)
    q_b = jnp.einsum("td,dgc->gtc", normed, q_turned, preferred_element_type=jnp.float32)
    query = (q_a * cos_q[None] + q_b * sin_q[None]).astype(jnp.bfloat16)

    kv_weight = key_value_weight.reshape(model_width, width)
    k_turned = jnp.concatenate(
        [turned_columns(kv_weight[:, :head_size]), jnp.zeros_like(kv_weight[:, head_size:])],
        axis=1,
    )
    ones_lanes = jnp.ones((token_count, width - head_size), jnp.float32)
    cos_k = jnp.concatenate([cos_part, ones_lanes], axis=1)
    sin_k = jnp.concatenate([sin_part, no_lanes], axis=1)
    kv_a = jnp.dot(normed, kv_weight, preferred_element_type=jnp.float32)
    kv_b = jnp.dot(normed, k_turned, preferred_element_type=jnp.float32)
    newkv = (kv_a * cos_k + kv_b * sin_k).astype(jnp.bfloat16)

    row_ids = jnp.arange(token_count, dtype=jnp.int32)
    offsets = jnp.arange(WIN, dtype=jnp.int32)
    select = (row_ids[:, None, None] == starts[None, :, None] + offsets[None, None, :]) & (
        offsets[None, None, :] < counts[None, :, None]
    )
    select = select.astype(jnp.bfloat16).reshape(token_count, req_n * WIN)
    q_win = jnp.einsum("tw,gtc->gwc", select, query, preferred_element_type=jnp.float32)
    q_win = q_win.astype(jnp.bfloat16).reshape(groups, req_n, WIN, width)
    nkv_win = jnp.einsum("tw,tc->wc", select, newkv, preferred_element_type=jnp.float32)
    nkv_win = nkv_win.astype(jnp.bfloat16).reshape(req_n, WIN, width)
    out_win = attention(counts, q_win, kv_cache, nkv_win)
    out_win = out_win[..., head_size:].reshape(groups, req_n * WIN, head_size)
    attn_rows = jnp.einsum("tw,gwc->gtc", select, out_win, preferred_element_type=jnp.float32)
    attn_rows = attn_rows.astype(jnp.bfloat16)
    n_head = lax.axis_size("head")
    per_block = routes.shape[0]
    row_start = lax.axis_index("head") * per_block
    leaving = jnp.transpose(attn_rows.reshape(groups, n_head, per_block, head_size), (1, 0, 2, 3))
    arriving = lax.all_to_all(leaving, "head", split_axis=0, concat_axis=0, tiled=True)
    o_weight = o_weight_all.reshape(n_head, groups, head_size, model_width)
    summed = jnp.einsum(
        "hgtc,hgcd->td", arriving, o_weight, preferred_element_type=jnp.float32
    )
    base_rows = lax.dynamic_slice_in_dim(whole, row_start, per_block, 0)
    resid = base_rows.astype(jnp.float32) + summed
    moe_in = norm_rows(resid, norm_moe).astype(jnp.bfloat16)
    capacity = per_block // 2
    expert_ids = jnp.arange(EXPERTS, dtype=jnp.int32)
    onehot = (routes.reshape(-1)[:, None] == expert_ids[None, :]).astype(jnp.bfloat16)
    pair_count = onehot.shape[0]
    chunk = 32
    lower = (
        jnp.arange(chunk, dtype=jnp.int32)[:, None] > jnp.arange(chunk, dtype=jnp.int32)[None, :]
    ).astype(jnp.bfloat16)
    pieces = onehot.reshape(pair_count // chunk, chunk, EXPERTS)
    within = jnp.einsum("ij,cje->cie", lower, pieces, preferred_element_type=jnp.float32)
    piece_total = jnp.sum(pieces.astype(jnp.float32), axis=1)
    piece_lower = (
        jnp.arange(pair_count // chunk, dtype=jnp.int32)[:, None]
        > jnp.arange(pair_count // chunk, dtype=jnp.int32)[None, :]
    ).astype(jnp.float32)
    earlier = jnp.dot(piece_lower, piece_total, precision=lax.Precision.HIGHEST)
    before = (within + earlier[:, None, :]).reshape(pair_count, EXPERTS)
    rank_in = jnp.sum(before * onehot.astype(jnp.float32), axis=1).astype(jnp.int32)
    slot_ids = (routes.reshape(-1) * capacity + rank_in).reshape(per_block, TOPK)
    slot_range = jnp.arange(EXPERTS * capacity, dtype=jnp.int32)
    hits = slot_ids[:, :, None] == slot_range[None, None, :]
    send = jnp.any(hits, axis=1).astype(jnp.bfloat16)
    combine = jnp.sum(jnp.where(hits, route_gain[:, :, None], 0.0), axis=1)
    combine_hi = combine.astype(jnp.bfloat16)
    combine_lo = (combine - combine_hi.astype(jnp.float32)).astype(jnp.bfloat16)
    req_count = lax.axis_size("req")
    per_req = w_down.shape[0]
    ff_width = w_down.shape[1]
    outgoing = lax.dot_general(
        send, moe_in, (((0,), (0,)), ((), ())), preferred_element_type=jnp.float32
    ).astype(jnp.bfloat16)
    outgoing = outgoing.reshape(req_count, per_req, capacity, model_width)
    gate_up = jnp.einsum(
        "sncd,ndf->sncf",
        lax.all_to_all(outgoing, "req", split_axis=0, concat_axis=0, tiled=True),
        w_gate_up,
        preferred_element_type=jnp.float32,
    )
    hidden = (jax.nn.silu(gate_up[..., :ff_width]) * gate_up[..., ff_width:]).astype(jnp.bfloat16)
    produced = jnp.einsum(
        "sncf,nfd->sncd", hidden, w_down, preferred_element_type=jnp.float32
    ).astype(jnp.bfloat16)
    arrived = lax.all_to_all(produced, "req", split_axis=0, concat_axis=0, tiled=True)
    arrived = arrived.reshape(EXPERTS * capacity, model_width)
    moe_sum = jnp.dot(combine_hi, arrived, preferred_element_type=jnp.float32) + jnp.dot(
        combine_lo, arrived, preferred_element_type=jnp.float32
    )
    return (resid + moe_sum).astype(jnp.bfloat16)


def solution(mesh):
    in_specs = (
        P("req", "head"),
        P("req", None),
        P("req", "head", None, None),
        P(),
        P(None, "head", None),
        P(None, "head", None),
        P("head", None, None),
        P(),
        P(("req", "head"), None),
        P(("req", "head"), None),
        P("req", None, None),
        P("req", None, None),
    )
    out_specs = P(("req", "head"), None)
    return jax.shard_map(local, mesh=mesh, in_specs=in_specs, out_specs=out_specs, check_vma=False)
```

```python
import math

import jax
import jax.numpy as jnp
from jax import lax
from jax.experimental import pallas as pl
from jax.experimental.pallas import tpu as pltpu
from jax.sharding import PartitionSpec as P

EXPERTS = 32
TOPK = 8
RATIO = 15
WIN = 512
TQ = 256
TK = 1536


floor_score = -1e30


def norm_rows(value_rows, gain_row):
    mean_square = jnp.mean(value_rows * value_rows, axis=-1, keepdims=True)
    return value_rows * lax.rsqrt(mean_square + 1e-05) * gain_row


def rope_tables(position, head_size):
    half_size = head_size // 2
    inverse = jnp.exp(
        jnp.arange(half_size, dtype=jnp.float32) * (-2.0 * math.log(10000.0) / head_size)
    )
    angles = position.astype(jnp.float32)[:, None] * inverse[None, :]
    angles = jnp.concatenate([angles, angles], axis=1)
    return (jnp.cos(angles), jnp.sin(angles))


def rotate(vectors, cos_part, sin_part):
    half_size = vectors.shape[-1] // 2
    turned = jnp.concatenate([-vectors[..., half_size:], vectors[..., :half_size]], axis=-1)
    return vectors * cos_part + turned * sin_part


def request_layout(counts, token_count, cache_ratio):
    end_rows = jnp.cumsum(counts)
    starts = end_rows - counts
    row_ids = jnp.arange(token_count, dtype=jnp.int32)
    segment = jnp.sum((row_ids[:, None] >= end_rows[None, :]).astype(jnp.int32), axis=1)
    member = (segment[:, None] == jnp.arange(counts.shape[0], dtype=jnp.int32)[None, :]).astype(
        jnp.int32
    )
    row_begin = jnp.sum(member * starts[None, :], axis=1)
    own_count = jnp.sum(member * counts[None, :], axis=1)
    position = cache_ratio * own_count + row_ids - row_begin
    return (starts, position)


def project(normed, query_weight, key_value_weight, position):
    token_count, model_width = normed.shape
    kv_heads = key_value_weight.shape[1]
    head_size = key_value_weight.shape[2] // 2
    group_size = query_weight.shape[2] // head_size
    query = jnp.dot(
        normed, query_weight.reshape(model_width, -1), preferred_element_type=jnp.float32
    )
    query = query.reshape(token_count, kv_heads, group_size, head_size)
    keyval = jnp.dot(
        normed, key_value_weight.reshape(model_width, -1), preferred_element_type=jnp.float32
    )
    keyval = keyval.reshape(token_count, kv_heads, 2 * head_size)
    cos_part, sin_part = rope_tables(position, head_size)
    query = rotate(query, cos_part[:, None, None, :], sin_part[:, None, None, :])
    query = (query * (1.0 / math.sqrt(head_size))).astype(jnp.bfloat16)
    new_key = rotate(keyval[..., :head_size], cos_part[:, None, :], sin_part[:, None, :]).astype(
        jnp.bfloat16
    )
    new_value = keyval[..., head_size:].astype(jnp.bfloat16)
    return (query, new_key, new_value)


def attn_kernel(counts_ref, q_ref, kv_ref, nkv_ref, o_ref, m_sc, l_sc, acc_sc):
    j = pl.program_id(0)
    qi = pl.program_id(1)
    kb = pl.program_id(2)
    last = pl.num_programs(2) - 1
    count = counts_ref[j]
    cached = RATIO * count
    groups, tq, width = q_ref.shape[0], q_ref.shape[2], q_ref.shape[3]
    tk = kv_ref.shape[2]
    win = nkv_ref.shape[1]
    tile_ok = qi * tq < count

    @pl.when(kb == 0)
    def _():
        m_sc[...] = jnp.full(m_sc.shape, floor_score, jnp.float32)
        l_sc[...] = jnp.zeros(l_sc.shape, jnp.float32)
        acc_sc[...] = jnp.zeros(acc_sc.shape, jnp.float32)

    def absorb(rows, mask):
        q = q_ref[:, 0].reshape(groups * tq, width)
        s = lax.dot_general(
            q, rows, (((1,), (1,)), ((), ())), preferred_element_type=jnp.float32
        )
        s = s.reshape(groups, tq, rows.shape[0])
        if mask is not None:
            s = jnp.where(mask, s, floor_score)
        m_old = m_sc[...]
        m_new = jnp.maximum(m_old, jnp.max(s, axis=-1, keepdims=True))
        alpha = jnp.exp(m_old - m_new)
        p = jnp.exp(s - m_new)
        l_sc[...] = l_sc[...] * alpha + jnp.sum(p, axis=-1, keepdims=True)
        pv = jnp.dot(
            p.astype(jnp.bfloat16).reshape(groups * tq, rows.shape[0]),
            rows,
            preferred_element_type=jnp.float32,
        )
        acc_sc[...] = acc_sc[...] * alpha + pv.reshape(groups, tq, width)
        m_sc[...] = m_new

    @pl.when(tile_ok & (kb == 0))
    def _():
        row = qi * tq + lax.broadcasted_iota(jnp.int32, (1, tq, win), 1)
        col = lax.broadcasted_iota(jnp.int32, (1, tq, win), 2)
        absorb(nkv_ref[0], col <= row)

    @pl.when(tile_ok & (kb > 0) & ((kb - 1) * tk < cached))
    def _():
        col = (kb - 1) * tk + lax.broadcasted_iota(jnp.int32, (1, 1, tk), 2)
        absorb(kv_ref[0, 0], col < cached)

    @pl.when(kb == last)
    def _():
        total = l_sc[...]
        total = jnp.where(total > 0.0, total, 1.0)
        o_ref[:, 0] = (acc_sc[...] / total).astype(o_ref.dtype)


def attention(counts, q_win, kv_cache, nkv_win):
    groups, req_n, win, width = q_win.shape
    cache_len = kv_cache.shape[2]
    n_tiles = win // TQ
    n_blocks = cache_len // TK

    def q_map(j, qi, kb, cnt):
        tiles = (cnt[j] + TQ - 1) // TQ
        return (0, j, jnp.minimum(qi, tiles - 1), 0)

    def kv_map(j, qi, kb, cnt):
        tiles = (cnt[j] + TQ - 1) // TQ
        blocks = (RATIO * cnt[j] + TK - 1) // TK
        inner = jnp.clip(kb - 1, 0, blocks - 1)
        return (j, 0, jnp.where(qi < tiles, inner, blocks - 1), 0)

    grid_spec = pltpu.PrefetchScalarGridSpec(
        num_scalar_prefetch=1,
        grid=(req_n, n_tiles, n_blocks + 1),
        in_specs=[
            pl.BlockSpec((groups, 1, TQ, width), q_map),
            pl.BlockSpec((1, 1, TK, width), kv_map),
            pl.BlockSpec((1, win, width), lambda j, qi, kb, cnt: (j, 0, 0)),
        ],
        out_specs=pl.BlockSpec((groups, 1, TQ, width), lambda j, qi, kb, cnt: (0, j, qi, 0)),
        scratch_shapes=[
            pltpu.VMEM((groups, TQ, 1), jnp.float32),
            pltpu.VMEM((groups, TQ, 1), jnp.float32),
            pltpu.VMEM((groups, TQ, width), jnp.float32),
        ],
    )
    return pl.pallas_call(
        attn_kernel,
        grid_spec=grid_spec,
        out_shape=jax.ShapeDtypeStruct(q_win.shape, jnp.bfloat16),
        compiler_params=pltpu.CompilerParams(
            dimension_semantics=("arbitrary", "arbitrary", "arbitrary")
        ),
    )(counts, q_win, kv_cache, nkv_win)


def turned_columns(weight):
    half = weight.shape[-1] // 2
    return jnp.concatenate([-weight[..., half:], weight[..., :half]], axis=-1)


def local(
    tokens,
    new_counts,
    kv_cache,
    norm_attn,
    query_weight,
    key_value_weight,
    output_weight,
    norm_moe,
    routes,
    route_gain,
    w_gate_up,
    w_down,
):
    whole = lax.all_gather(tokens, "head", axis=1, tiled=True)
    o_weight_all = lax.all_gather(output_weight, "head", axis=0, tiled=True)
    token_count, model_width = whole.shape
    normed = norm_rows(whole.astype(jnp.float32), norm_attn).astype(jnp.bfloat16)
    counts = new_counts[0]
    starts, position = request_layout(counts, token_count, RATIO)
    req_n = counts.shape[0]
    head_size = key_value_weight.shape[2] // 2
    groups = query_weight.shape[2] // head_size
    width = 2 * head_size

    cos_part, sin_part = rope_tables(position, head_size)
    scale = 1.0 / math.sqrt(head_size)
    no_lanes = jnp.zeros((token_count, width - head_size), jnp.float32)
    cos_q = jnp.concatenate([cos_part * scale, no_lanes], axis=1)
    sin_q = jnp.concatenate([sin_part * scale, no_lanes], axis=1)
    q_weight = query_weight.reshape(model_width, groups, head_size)
    no_cols = jnp.zeros((model_width, groups, width - head_size), q_weight.dtype)
    q_plain = jnp.concatenate([q_weight, no_cols], axis=-1)
    q_turned = jnp.concatenate([turned_columns(q_weight), no_cols], axis=-1)
    q_a = jnp.einsum("td,dgc->gtc", normed, q_plain, preferred_element_type=jnp.float32)
    q_b = jnp.einsum("td,dgc->gtc", normed, q_turned, preferred_element_type=jnp.float32)
    query = (q_a * cos_q[None] + q_b * sin_q[None]).astype(jnp.bfloat16)

    kv_weight = key_value_weight.reshape(model_width, width)
    k_turned = jnp.concatenate(
        [turned_columns(kv_weight[:, :head_size]), jnp.zeros_like(kv_weight[:, head_size:])],
        axis=1,
    )
    ones_lanes = jnp.ones((token_count, width - head_size), jnp.float32)
    cos_k = jnp.concatenate([cos_part, ones_lanes], axis=1)
    sin_k = jnp.concatenate([sin_part, no_lanes], axis=1)
    kv_a = jnp.dot(normed, kv_weight, preferred_element_type=jnp.float32)
    kv_b = jnp.dot(normed, k_turned, preferred_element_type=jnp.float32)
    newkv = (kv_a * cos_k + kv_b * sin_k).astype(jnp.bfloat16)

    row_ids = jnp.arange(token_count, dtype=jnp.int32)
    offsets = jnp.arange(WIN, dtype=jnp.int32)
    select = (row_ids[:, None, None] == starts[None, :, None] + offsets[None, None, :]) & (
        offsets[None, None, :] < counts[None, :, None]
    )
    select = select.astype(jnp.bfloat16).reshape(token_count, req_n * WIN)
    q_win = jnp.einsum("tw,gtc->gwc", select, query, preferred_element_type=jnp.float32)
    q_win = q_win.astype(jnp.bfloat16).reshape(groups, req_n, WIN, width)
    nkv_win = jnp.einsum("tw,tc->wc", select, newkv, preferred_element_type=jnp.float32)
    nkv_win = nkv_win.astype(jnp.bfloat16).reshape(req_n, WIN, width)
    out_win = attention(counts, q_win, kv_cache, nkv_win)
    out_win = out_win[..., head_size:].reshape(groups, req_n * WIN, head_size)
    attn_rows = jnp.einsum("tw,gwc->gtc", select, out_win, preferred_element_type=jnp.float32)
    attn_rows = attn_rows.astype(jnp.bfloat16)
    n_head = lax.axis_size("head")
    per_block = routes.shape[0]
    row_start = lax.axis_index("head") * per_block
    leaving = jnp.transpose(attn_rows.reshape(groups, n_head, per_block, head_size), (1, 0, 2, 3))
    arriving = lax.all_to_all(leaving, "head", split_axis=0, concat_axis=0, tiled=True)
    o_weight = o_weight_all.reshape(n_head, groups, head_size, model_width)
    summed = jnp.einsum(
        "hgtc,hgcd->td", arriving, o_weight, preferred_element_type=jnp.float32
    )
    base_rows = lax.dynamic_slice_in_dim(whole, row_start, per_block, 0)
    resid = base_rows.astype(jnp.float32) + summed
    moe_in = norm_rows(resid, norm_moe).astype(jnp.bfloat16)
    capacity = per_block // 2
    expert_ids = jnp.arange(EXPERTS, dtype=jnp.int32)
    onehot = (routes.reshape(-1)[:, None] == expert_ids[None, :]).astype(jnp.bfloat16)
    pair_count = onehot.shape[0]
    chunk = 32
    lower = (
        jnp.arange(chunk, dtype=jnp.int32)[:, None] > jnp.arange(chunk, dtype=jnp.int32)[None, :]
    ).astype(jnp.bfloat16)
    pieces = onehot.reshape(pair_count // chunk, chunk, EXPERTS)
    within = jnp.einsum("ij,cje->cie", lower, pieces, preferred_element_type=jnp.float32)
    piece_total = jnp.sum(pieces.astype(jnp.float32), axis=1)
    piece_lower = (
        jnp.arange(pair_count // chunk, dtype=jnp.int32)[:, None]
        > jnp.arange(pair_count // chunk, dtype=jnp.int32)[None, :]
    ).astype(jnp.float32)
    earlier = jnp.dot(piece_lower, piece_total, precision=lax.Precision.HIGHEST)
    before = (within + earlier[:, None, :]).reshape(pair_count, EXPERTS)
    rank_in = jnp.sum(before * onehot.astype(jnp.float32), axis=1).astype(jnp.int32)
    slot_ids = (routes.reshape(-1) * capacity + rank_in).reshape(per_block, TOPK)
    slot_range = jnp.arange(EXPERTS * capacity, dtype=jnp.int32)
    hits = slot_ids[:, :, None] == slot_range[None, None, :]
    send = jnp.any(hits, axis=1).astype(jnp.bfloat16)
    combine = jnp.sum(jnp.where(hits, route_gain[:, :, None], 0.0), axis=1)
    combine_hi = combine.astype(jnp.bfloat16)
    combine_lo = (combine - combine_hi.astype(jnp.float32)).astype(jnp.bfloat16)
    req_count = lax.axis_size("req")
    per_req = w_down.shape[0]
    ff_width = w_down.shape[1]
    send = send.reshape(per_block, req_count, per_req, capacity)
    combine_hi = combine_hi.reshape(per_block, req_count, per_req, capacity)
    combine_lo = combine_lo.reshape(per_block, req_count, per_req, capacity)
    moe_sum = jnp.zeros((per_block, model_width), jnp.float32)
    for e in range(per_req):
        send_e = send[:, :, e, :].reshape(per_block, req_count * capacity)
        outgoing = lax.dot_general(
            send_e, moe_in, (((0,), (0,)), ((), ())), preferred_element_type=jnp.float32
        ).astype(jnp.bfloat16)
        outgoing = outgoing.reshape(req_count, capacity, model_width)
        landed = lax.all_to_all(outgoing, "req", split_axis=0, concat_axis=0, tiled=True)
        gate_up = jnp.einsum(
            "scd,df->scf", landed, w_gate_up[e], preferred_element_type=jnp.float32
        )
        hidden = (jax.nn.silu(gate_up[..., :ff_width]) * gate_up[..., ff_width:]).astype(
            jnp.bfloat16
        )
        produced = jnp.einsum(
            "scf,fd->scd", hidden, w_down[e], preferred_element_type=jnp.float32
        ).astype(jnp.bfloat16)
        arrived = lax.all_to_all(produced, "req", split_axis=0, concat_axis=0, tiled=True)
        arrived = arrived.reshape(req_count * capacity, model_width)
        hi_e = combine_hi[:, :, e, :].reshape(per_block, req_count * capacity)
        lo_e = combine_lo[:, :, e, :].reshape(per_block, req_count * capacity)
        moe_sum = moe_sum + (
            jnp.dot(hi_e, arrived, preferred_element_type=jnp.float32)
            + jnp.dot(lo_e, arrived, preferred_element_type=jnp.float32)
        )
    return (resid + moe_sum).astype(jnp.bfloat16)


def solution(mesh):
    in_specs = (
        P("req", "head"),
        P("req", None),
        P("req", "head", None, None),
        P(),
        P(None, "head", None),
        P(None, "head", None),
        P("head", None, None),
        P(),
        P(("req", "head"), None),
        P(("req", "head"), None),
        P("req", None, None),
        P("req", None, None),
    )
    out_specs = P(("req", "head"), None)
    return jax.shard_map(local, mesh=mesh, in_specs=in_specs, out_specs=out_specs, check_vma=False)
```

```python
import math

import jax
import jax.numpy as jnp
from jax import lax
from jax.experimental import pallas as pl
from jax.experimental.pallas import tpu as pltpu
from jax.sharding import PartitionSpec as P

EXPERTS = 32
TOPK = 8
RATIO = 15
WIN = 512
TQ = 128
TK = 1536


floor_score = -1e30


def norm_rows(value_rows, gain_row):
    mean_square = jnp.mean(value_rows * value_rows, axis=-1, keepdims=True)
    return value_rows * lax.rsqrt(mean_square + 1e-05) * gain_row


def rope_tables(position, head_size):
    half_size = head_size // 2
    inverse = jnp.exp(
        jnp.arange(half_size, dtype=jnp.float32) * (-2.0 * math.log(10000.0) / head_size)
    )
    angles = position.astype(jnp.float32)[:, None] * inverse[None, :]
    angles = jnp.concatenate([angles, angles], axis=1)
    return (jnp.cos(angles), jnp.sin(angles))


def rotate(vectors, cos_part, sin_part):
    half_size = vectors.shape[-1] // 2
    turned = jnp.concatenate([-vectors[..., half_size:], vectors[..., :half_size]], axis=-1)
    return vectors * cos_part + turned * sin_part


def request_layout(counts, token_count, cache_ratio):
    end_rows = jnp.cumsum(counts)
    starts = end_rows - counts
    row_ids = jnp.arange(token_count, dtype=jnp.int32)
    segment = jnp.sum((row_ids[:, None] >= end_rows[None, :]).astype(jnp.int32), axis=1)
    member = (segment[:, None] == jnp.arange(counts.shape[0], dtype=jnp.int32)[None, :]).astype(
        jnp.int32
    )
    row_begin = jnp.sum(member * starts[None, :], axis=1)
    own_count = jnp.sum(member * counts[None, :], axis=1)
    position = cache_ratio * own_count + row_ids - row_begin
    return (starts, position)


def project(normed, query_weight, key_value_weight, position):
    token_count, model_width = normed.shape
    kv_heads = key_value_weight.shape[1]
    head_size = key_value_weight.shape[2] // 2
    group_size = query_weight.shape[2] // head_size
    query = jnp.dot(
        normed, query_weight.reshape(model_width, -1), preferred_element_type=jnp.float32
    )
    query = query.reshape(token_count, kv_heads, group_size, head_size)
    keyval = jnp.dot(
        normed, key_value_weight.reshape(model_width, -1), preferred_element_type=jnp.float32
    )
    keyval = keyval.reshape(token_count, kv_heads, 2 * head_size)
    cos_part, sin_part = rope_tables(position, head_size)
    query = rotate(query, cos_part[:, None, None, :], sin_part[:, None, None, :])
    query = (query * (1.0 / math.sqrt(head_size))).astype(jnp.bfloat16)
    new_key = rotate(keyval[..., :head_size], cos_part[:, None, :], sin_part[:, None, :]).astype(
        jnp.bfloat16
    )
    new_value = keyval[..., head_size:].astype(jnp.bfloat16)
    return (query, new_key, new_value)


def attn_kernel(counts_ref, q_ref, kv_ref, nkv_ref, o_ref, m_sc, l_sc, acc_sc):
    j = pl.program_id(0)
    qi = pl.program_id(1)
    kb = pl.program_id(2)
    last = pl.num_programs(2) - 1
    count = counts_ref[j]
    cached = RATIO * count
    groups, tq, width = q_ref.shape[0], q_ref.shape[2], q_ref.shape[3]
    tk = kv_ref.shape[2]
    win = nkv_ref.shape[1]
    tile_ok = qi * tq < count

    @pl.when(kb == 0)
    def _():
        m_sc[...] = jnp.full(m_sc.shape, floor_score, jnp.float32)
        l_sc[...] = jnp.zeros(l_sc.shape, jnp.float32)
        acc_sc[...] = jnp.zeros(acc_sc.shape, jnp.float32)

    def absorb(rows, mask):
        q = q_ref[:, 0].reshape(groups * tq, width)
        s = lax.dot_general(
            q, rows, (((1,), (1,)), ((), ())), preferred_element_type=jnp.float32
        )
        s = s.reshape(groups, tq, rows.shape[0])
        if mask is not None:
            s = jnp.where(mask, s, floor_score)
        m_old = m_sc[...]
        m_new = jnp.maximum(m_old, jnp.max(s, axis=-1, keepdims=True))
        alpha = jnp.exp(m_old - m_new)
        p = jnp.exp(s - m_new)
        l_sc[...] = l_sc[...] * alpha + jnp.sum(p, axis=-1, keepdims=True)
        pv = jnp.dot(
            p.astype(jnp.bfloat16).reshape(groups * tq, rows.shape[0]),
            rows,
            preferred_element_type=jnp.float32,
        )
        acc_sc[...] = acc_sc[...] * alpha + pv.reshape(groups, tq, width)
        m_sc[...] = m_new

    @pl.when(tile_ok & (kb == 0))
    def _():
        row = qi * tq + lax.broadcasted_iota(jnp.int32, (1, tq, win), 1)
        col = lax.broadcasted_iota(jnp.int32, (1, tq, win), 2)
        absorb(nkv_ref[0], col <= row)

    @pl.when(tile_ok & (kb > 0) & ((kb - 1) * tk < cached))
    def _():
        col = (kb - 1) * tk + lax.broadcasted_iota(jnp.int32, (1, 1, tk), 2)
        absorb(kv_ref[0, 0], col < cached)

    @pl.when(kb == last)
    def _():
        total = l_sc[...]
        total = jnp.where(total > 0.0, total, 1.0)
        o_ref[:, 0] = (acc_sc[...] / total).astype(o_ref.dtype)


def attention(counts, q_win, kv_cache, nkv_win):
    groups, req_n, win, width = q_win.shape
    cache_len = kv_cache.shape[2]
    n_tiles = win // TQ
    n_blocks = cache_len // TK

    def q_map(j, qi, kb, cnt):
        tiles = (cnt[j] + TQ - 1) // TQ
        return (0, j, jnp.minimum(qi, tiles - 1), 0)

    def kv_map(j, qi, kb, cnt):
        tiles = (cnt[j] + TQ - 1) // TQ
        blocks = (RATIO * cnt[j] + TK - 1) // TK
        inner = jnp.clip(kb - 1, 0, blocks - 1)
        return (j, 0, jnp.where(qi < tiles, inner, blocks - 1), 0)

    grid_spec = pltpu.PrefetchScalarGridSpec(
        num_scalar_prefetch=1,
        grid=(req_n, n_tiles, n_blocks + 1),
        in_specs=[
            pl.BlockSpec((groups, 1, TQ, width), q_map),
            pl.BlockSpec((1, 1, TK, width), kv_map),
            pl.BlockSpec((1, win, width), lambda j, qi, kb, cnt: (j, 0, 0)),
        ],
        out_specs=pl.BlockSpec((groups, 1, TQ, width), lambda j, qi, kb, cnt: (0, j, qi, 0)),
        scratch_shapes=[
            pltpu.VMEM((groups, TQ, 1), jnp.float32),
            pltpu.VMEM((groups, TQ, 1), jnp.float32),
            pltpu.VMEM((groups, TQ, width), jnp.float32),
        ],
    )
    return pl.pallas_call(
        attn_kernel,
        grid_spec=grid_spec,
        out_shape=jax.ShapeDtypeStruct(q_win.shape, jnp.bfloat16),
        compiler_params=pltpu.CompilerParams(
            dimension_semantics=("arbitrary", "arbitrary", "arbitrary")
        ),
    )(counts, q_win, kv_cache, nkv_win)


def turned_columns(weight):
    half = weight.shape[-1] // 2
    return jnp.concatenate([-weight[..., half:], weight[..., :half]], axis=-1)


def local(
    tokens,
    new_counts,
    kv_cache,
    norm_attn,
    query_weight,
    key_value_weight,
    output_weight,
    norm_moe,
    routes,
    route_gain,
    w_gate_up,
    w_down,
):
    whole = lax.all_gather(tokens, "head", axis=1, tiled=True)
    o_weight_all = lax.all_gather(output_weight, "head", axis=0, tiled=True)
    token_count, model_width = whole.shape
    normed = norm_rows(whole.astype(jnp.float32), norm_attn).astype(jnp.bfloat16)
    counts = new_counts[0]
    starts, position = request_layout(counts, token_count, RATIO)
    req_n = counts.shape[0]
    head_size = key_value_weight.shape[2] // 2
    groups = query_weight.shape[2] // head_size
    width = 2 * head_size

    cos_part, sin_part = rope_tables(position, head_size)
    scale = 1.0 / math.sqrt(head_size)
    no_lanes = jnp.zeros((token_count, width - head_size), jnp.float32)
    cos_q = jnp.concatenate([cos_part * scale, no_lanes], axis=1)
    sin_q = jnp.concatenate([sin_part * scale, no_lanes], axis=1)
    q_weight = query_weight.reshape(model_width, groups, head_size)
    no_cols = jnp.zeros((model_width, groups, width - head_size), q_weight.dtype)
    q_plain = jnp.concatenate([q_weight, no_cols], axis=-1)
    q_turned = jnp.concatenate([turned_columns(q_weight), no_cols], axis=-1)
    q_a = jnp.einsum("td,dgc->gtc", normed, q_plain, preferred_element_type=jnp.float32)
    q_b = jnp.einsum("td,dgc->gtc", normed, q_turned, preferred_element_type=jnp.float32)
    query = (q_a * cos_q[None] + q_b * sin_q[None]).astype(jnp.bfloat16)

    kv_weight = key_value_weight.reshape(model_width, width)
    k_turned = jnp.concatenate(
        [turned_columns(kv_weight[:, :head_size]), jnp.zeros_like(kv_weight[:, head_size:])],
        axis=1,
    )
    ones_lanes = jnp.ones((token_count, width - head_size), jnp.float32)
    cos_k = jnp.concatenate([cos_part, ones_lanes], axis=1)
    sin_k = jnp.concatenate([sin_part, no_lanes], axis=1)
    kv_a = jnp.dot(normed, kv_weight, preferred_element_type=jnp.float32)
    kv_b = jnp.dot(normed, k_turned, preferred_element_type=jnp.float32)
    newkv = (kv_a * cos_k + kv_b * sin_k).astype(jnp.bfloat16)

    row_ids = jnp.arange(token_count, dtype=jnp.int32)
    offsets = jnp.arange(WIN, dtype=jnp.int32)
    select = (row_ids[:, None, None] == starts[None, :, None] + offsets[None, None, :]) & (
        offsets[None, None, :] < counts[None, :, None]
    )
    select = select.astype(jnp.bfloat16).reshape(token_count, req_n * WIN)
    q_win = jnp.einsum("tw,gtc->gwc", select, query, preferred_element_type=jnp.float32)
    q_win = q_win.astype(jnp.bfloat16).reshape(groups, req_n, WIN, width)
    nkv_win = jnp.einsum("tw,tc->wc", select, newkv, preferred_element_type=jnp.float32)
    nkv_win = nkv_win.astype(jnp.bfloat16).reshape(req_n, WIN, width)
    out_win = attention(counts, q_win, kv_cache, nkv_win)
    out_win = out_win[..., head_size:].reshape(groups, req_n * WIN, head_size)
    attn_rows = jnp.einsum("tw,gwc->gtc", select, out_win, preferred_element_type=jnp.float32)
    attn_rows = attn_rows.astype(jnp.bfloat16)
    n_head = lax.axis_size("head")
    per_block = routes.shape[0]
    row_start = lax.axis_index("head") * per_block
    leaving = jnp.transpose(attn_rows.reshape(groups, n_head, per_block, head_size), (1, 0, 2, 3))
    arriving = lax.all_to_all(leaving, "head", split_axis=0, concat_axis=0, tiled=True)
    o_weight = o_weight_all.reshape(n_head, groups, head_size, model_width)
    summed = jnp.einsum(
        "hgtc,hgcd->td", arriving, o_weight, preferred_element_type=jnp.float32
    )
    base_rows = lax.dynamic_slice_in_dim(whole, row_start, per_block, 0)
    resid = base_rows.astype(jnp.float32) + summed
    moe_in = norm_rows(resid, norm_moe).astype(jnp.bfloat16)
    capacity = per_block // 2
    expert_ids = jnp.arange(EXPERTS, dtype=jnp.int32)
    onehot = (routes.reshape(-1)[:, None] == expert_ids[None, :]).astype(jnp.bfloat16)
    pair_count = onehot.shape[0]
    chunk = 32
    lower = (
        jnp.arange(chunk, dtype=jnp.int32)[:, None] > jnp.arange(chunk, dtype=jnp.int32)[None, :]
    ).astype(jnp.bfloat16)
    pieces = onehot.reshape(pair_count // chunk, chunk, EXPERTS)
    within = jnp.einsum("ij,cje->cie", lower, pieces, preferred_element_type=jnp.float32)
    piece_total = jnp.sum(pieces.astype(jnp.float32), axis=1)
    piece_lower = (
        jnp.arange(pair_count // chunk, dtype=jnp.int32)[:, None]
        > jnp.arange(pair_count // chunk, dtype=jnp.int32)[None, :]
    ).astype(jnp.float32)
    earlier = jnp.dot(piece_lower, piece_total, precision=lax.Precision.HIGHEST)
    before = (within + earlier[:, None, :]).reshape(pair_count, EXPERTS)
    rank_in = jnp.sum(before * onehot.astype(jnp.float32), axis=1).astype(jnp.int32)
    slot_ids = (routes.reshape(-1) * capacity + rank_in).reshape(per_block, TOPK)
    slot_range = jnp.arange(EXPERTS * capacity, dtype=jnp.int32)
    hits = slot_ids[:, :, None] == slot_range[None, None, :]
    send = jnp.any(hits, axis=1).astype(jnp.bfloat16)
    combine = jnp.sum(jnp.where(hits, route_gain[:, :, None], 0.0), axis=1)
    combine_hi = combine.astype(jnp.bfloat16)
    combine_lo = (combine - combine_hi.astype(jnp.float32)).astype(jnp.bfloat16)
    req_count = lax.axis_size("req")
    per_req = w_down.shape[0]
    ff_width = w_down.shape[1]
    send = send.reshape(per_block, req_count, per_req, capacity)
    combine_hi = combine_hi.reshape(per_block, req_count, per_req, capacity)
    combine_lo = combine_lo.reshape(per_block, req_count, per_req, capacity)
    moe_sum = jnp.zeros((per_block, model_width), jnp.float32)
    for e in range(per_req):
        send_e = send[:, :, e, :].reshape(per_block, req_count * capacity)
        outgoing = lax.dot_general(
            send_e, moe_in, (((0,), (0,)), ((), ())), preferred_element_type=jnp.float32
        ).astype(jnp.bfloat16)
        outgoing = outgoing.reshape(req_count, capacity, model_width)
        landed = lax.all_to_all(outgoing, "req", split_axis=0, concat_axis=0, tiled=True)
        gate_up = jnp.einsum(
            "scd,df->scf", landed, w_gate_up[e], preferred_element_type=jnp.float32
        )
        hidden = (jax.nn.silu(gate_up[..., :ff_width]) * gate_up[..., ff_width:]).astype(
            jnp.bfloat16
        )
        produced = jnp.einsum(
            "scf,fd->scd", hidden, w_down[e], preferred_element_type=jnp.float32
        ).astype(jnp.bfloat16)
        arrived = lax.all_to_all(produced, "req", split_axis=0, concat_axis=0, tiled=True)
        arrived = arrived.reshape(req_count * capacity, model_width)
        hi_e = combine_hi[:, :, e, :].reshape(per_block, req_count * capacity)
        lo_e = combine_lo[:, :, e, :].reshape(per_block, req_count * capacity)
        moe_sum = moe_sum + (
            jnp.dot(hi_e, arrived, preferred_element_type=jnp.float32)
            + jnp.dot(lo_e, arrived, preferred_element_type=jnp.float32)
        )
    return (resid + moe_sum).astype(jnp.bfloat16)


def solution(mesh):
    in_specs = (
        P("req", "head"),
        P("req", None),
        P("req", "head", None, None),
        P(),
        P(None, "head", None),
        P(None, "head", None),
        P("head", None, None),
        P(),
        P(("req", "head"), None),
        P(("req", "head"), None),
        P("req", None, None),
        P("req", None, None),
    )
    out_specs = P(("req", "head"), None)
    return jax.shard_map(local, mesh=mesh, in_specs=in_specs, out_specs=out_specs, check_vma=False)
```

```python
import math

import jax
import jax.numpy as jnp
from jax import lax
from jax.experimental import pallas as pl
from jax.experimental.pallas import tpu as pltpu
from jax.sharding import PartitionSpec as P

EXPERTS = 32
TOPK = 8
RATIO = 15
WIN = 512
TQ = 256
TK = 2560


floor_score = -1e30


def norm_rows(value_rows, gain_row):
    mean_square = jnp.mean(value_rows * value_rows, axis=-1, keepdims=True)
    return value_rows * lax.rsqrt(mean_square + 1e-05) * gain_row


def rope_tables(position, head_size):
    half_size = head_size // 2
    inverse = jnp.exp(
        jnp.arange(half_size, dtype=jnp.float32) * (-2.0 * math.log(10000.0) / head_size)
    )
    angles = position.astype(jnp.float32)[:, None] * inverse[None, :]
    angles = jnp.concatenate([angles, angles], axis=1)
    return (jnp.cos(angles), jnp.sin(angles))


def rotate(vectors, cos_part, sin_part):
    half_size = vectors.shape[-1] // 2
    turned = jnp.concatenate([-vectors[..., half_size:], vectors[..., :half_size]], axis=-1)
    return vectors * cos_part + turned * sin_part


def request_layout(counts, token_count, cache_ratio):
    end_rows = jnp.cumsum(counts)
    starts = end_rows - counts
    row_ids = jnp.arange(token_count, dtype=jnp.int32)
    segment = jnp.sum((row_ids[:, None] >= end_rows[None, :]).astype(jnp.int32), axis=1)
    member = (segment[:, None] == jnp.arange(counts.shape[0], dtype=jnp.int32)[None, :]).astype(
        jnp.int32
    )
    row_begin = jnp.sum(member * starts[None, :], axis=1)
    own_count = jnp.sum(member * counts[None, :], axis=1)
    position = cache_ratio * own_count + row_ids - row_begin
    return (starts, position)


def project(normed, query_weight, key_value_weight, position):
    token_count, model_width = normed.shape
    kv_heads = key_value_weight.shape[1]
    head_size = key_value_weight.shape[2] // 2
    group_size = query_weight.shape[2] // head_size
    query = jnp.dot(
        normed, query_weight.reshape(model_width, -1), preferred_element_type=jnp.float32
    )
    query = query.reshape(token_count, kv_heads, group_size, head_size)
    keyval = jnp.dot(
        normed, key_value_weight.reshape(model_width, -1), preferred_element_type=jnp.float32
    )
    keyval = keyval.reshape(token_count, kv_heads, 2 * head_size)
    cos_part, sin_part = rope_tables(position, head_size)
    query = rotate(query, cos_part[:, None, None, :], sin_part[:, None, None, :])
    query = (query * (1.0 / math.sqrt(head_size))).astype(jnp.bfloat16)
    new_key = rotate(keyval[..., :head_size], cos_part[:, None, :], sin_part[:, None, :]).astype(
        jnp.bfloat16
    )
    new_value = keyval[..., head_size:].astype(jnp.bfloat16)
    return (query, new_key, new_value)


def attn_kernel(counts_ref, q_ref, kv_ref, nkv_ref, o_ref, m_sc, l_sc, acc_sc):
    j = pl.program_id(0)
    qi = pl.program_id(1)
    kb = pl.program_id(2)
    last = pl.num_programs(2) - 1
    count = counts_ref[j]
    cached = RATIO * count
    groups, tq, width = q_ref.shape[0], q_ref.shape[2], q_ref.shape[3]
    tk = kv_ref.shape[2]
    win = nkv_ref.shape[1]
    tile_ok = qi * tq < count

    @pl.when(kb == 0)
    def _():
        m_sc[...] = jnp.full(m_sc.shape, floor_score, jnp.float32)
        l_sc[...] = jnp.zeros(l_sc.shape, jnp.float32)
        acc_sc[...] = jnp.zeros(acc_sc.shape, jnp.float32)

    def absorb(rows, mask):
        q = q_ref[:, 0].reshape(groups * tq, width)
        s = lax.dot_general(
            q, rows, (((1,), (1,)), ((), ())), preferred_element_type=jnp.float32
        )
        s = s.reshape(groups, tq, rows.shape[0])
        if mask is not None:
            s = jnp.where(mask, s, floor_score)
        m_old = m_sc[...]
        m_new = jnp.maximum(m_old, jnp.max(s, axis=-1, keepdims=True))
        alpha = jnp.exp(m_old - m_new)
        p = jnp.exp(s - m_new)
        l_sc[...] = l_sc[...] * alpha + jnp.sum(p, axis=-1, keepdims=True)
        pv = jnp.dot(
            p.astype(jnp.bfloat16).reshape(groups * tq, rows.shape[0]),
            rows,
            preferred_element_type=jnp.float32,
        )
        acc_sc[...] = acc_sc[...] * alpha + pv.reshape(groups, tq, width)
        m_sc[...] = m_new

    @pl.when(tile_ok & (kb == 0))
    def _():
        row = qi * tq + lax.broadcasted_iota(jnp.int32, (1, tq, win), 1)
        col = lax.broadcasted_iota(jnp.int32, (1, tq, win), 2)
        absorb(nkv_ref[0], col <= row)

    @pl.when(tile_ok & (kb > 0) & ((kb - 1) * tk < cached))
    def _():
        col = (kb - 1) * tk + lax.broadcasted_iota(jnp.int32, (1, 1, tk), 2)
        absorb(kv_ref[0, 0], col < cached)

    @pl.when(kb == last)
    def _():
        total = l_sc[...]
        total = jnp.where(total > 0.0, total, 1.0)
        o_ref[:, 0] = (acc_sc[...] / total).astype(o_ref.dtype)


def attention(counts, q_win, kv_cache, nkv_win):
    groups, req_n, win, width = q_win.shape
    cache_len = kv_cache.shape[2]
    n_tiles = win // TQ
    n_blocks = cache_len // TK

    def q_map(j, qi, kb, cnt):
        tiles = (cnt[j] + TQ - 1) // TQ
        return (0, j, jnp.minimum(qi, tiles - 1), 0)

    def kv_map(j, qi, kb, cnt):
        tiles = (cnt[j] + TQ - 1) // TQ
        blocks = (RATIO * cnt[j] + TK - 1) // TK
        inner = jnp.clip(kb - 1, 0, blocks - 1)
        return (j, 0, jnp.where(qi < tiles, inner, blocks - 1), 0)

    grid_spec = pltpu.PrefetchScalarGridSpec(
        num_scalar_prefetch=1,
        grid=(req_n, n_tiles, n_blocks + 1),
        in_specs=[
            pl.BlockSpec((groups, 1, TQ, width), q_map),
            pl.BlockSpec((1, 1, TK, width), kv_map),
            pl.BlockSpec((1, win, width), lambda j, qi, kb, cnt: (j, 0, 0)),
        ],
        out_specs=pl.BlockSpec((groups, 1, TQ, width), lambda j, qi, kb, cnt: (0, j, qi, 0)),
        scratch_shapes=[
            pltpu.VMEM((groups, TQ, 1), jnp.float32),
            pltpu.VMEM((groups, TQ, 1), jnp.float32),
            pltpu.VMEM((groups, TQ, width), jnp.float32),
        ],
    )
    return pl.pallas_call(
        attn_kernel,
        grid_spec=grid_spec,
        out_shape=jax.ShapeDtypeStruct(q_win.shape, jnp.bfloat16),
        compiler_params=pltpu.CompilerParams(
            dimension_semantics=("arbitrary", "arbitrary", "arbitrary")
        ),
    )(counts, q_win, kv_cache, nkv_win)


def turned_columns(weight):
    half = weight.shape[-1] // 2
    return jnp.concatenate([-weight[..., half:], weight[..., :half]], axis=-1)


def local(
    tokens,
    new_counts,
    kv_cache,
    norm_attn,
    query_weight,
    key_value_weight,
    output_weight,
    norm_moe,
    routes,
    route_gain,
    w_gate_up,
    w_down,
):
    whole = lax.all_gather(tokens, "head", axis=1, tiled=True)
    o_weight_all = lax.all_gather(output_weight, "head", axis=0, tiled=True)
    token_count, model_width = whole.shape
    normed = norm_rows(whole.astype(jnp.float32), norm_attn).astype(jnp.bfloat16)
    counts = new_counts[0]
    starts, position = request_layout(counts, token_count, RATIO)
    req_n = counts.shape[0]
    head_size = key_value_weight.shape[2] // 2
    groups = query_weight.shape[2] // head_size
    width = 2 * head_size

    cos_part, sin_part = rope_tables(position, head_size)
    scale = 1.0 / math.sqrt(head_size)
    no_lanes = jnp.zeros((token_count, width - head_size), jnp.float32)
    cos_q = jnp.concatenate([cos_part * scale, no_lanes], axis=1)
    sin_q = jnp.concatenate([sin_part * scale, no_lanes], axis=1)
    q_weight = query_weight.reshape(model_width, groups, head_size)
    no_cols = jnp.zeros((model_width, groups, width - head_size), q_weight.dtype)
    q_plain = jnp.concatenate([q_weight, no_cols], axis=-1)
    q_turned = jnp.concatenate([turned_columns(q_weight), no_cols], axis=-1)
    q_a = jnp.einsum("td,dgc->gtc", normed, q_plain, preferred_element_type=jnp.float32)
    q_b = jnp.einsum("td,dgc->gtc", normed, q_turned, preferred_element_type=jnp.float32)
    query = (q_a * cos_q[None] + q_b * sin_q[None]).astype(jnp.bfloat16)

    kv_weight = key_value_weight.reshape(model_width, width)
    k_turned = jnp.concatenate(
        [turned_columns(kv_weight[:, :head_size]), jnp.zeros_like(kv_weight[:, head_size:])],
        axis=1,
    )
    ones_lanes = jnp.ones((token_count, width - head_size), jnp.float32)
    cos_k = jnp.concatenate([cos_part, ones_lanes], axis=1)
    sin_k = jnp.concatenate([sin_part, no_lanes], axis=1)
    kv_a = jnp.dot(normed, kv_weight, preferred_element_type=jnp.float32)
    kv_b = jnp.dot(normed, k_turned, preferred_element_type=jnp.float32)
    newkv = (kv_a * cos_k + kv_b * sin_k).astype(jnp.bfloat16)

    row_ids = jnp.arange(token_count, dtype=jnp.int32)
    offsets = jnp.arange(WIN, dtype=jnp.int32)
    select = (row_ids[:, None, None] == starts[None, :, None] + offsets[None, None, :]) & (
        offsets[None, None, :] < counts[None, :, None]
    )
    select = select.astype(jnp.bfloat16).reshape(token_count, req_n * WIN)
    q_win = jnp.einsum("tw,gtc->gwc", select, query, preferred_element_type=jnp.float32)
    q_win = q_win.astype(jnp.bfloat16).reshape(groups, req_n, WIN, width)
    nkv_win = jnp.einsum("tw,tc->wc", select, newkv, preferred_element_type=jnp.float32)
    nkv_win = nkv_win.astype(jnp.bfloat16).reshape(req_n, WIN, width)
    out_win = attention(counts, q_win, kv_cache, nkv_win)
    out_win = out_win[..., head_size:].reshape(groups, req_n * WIN, head_size)
    attn_rows = jnp.einsum("tw,gwc->gtc", select, out_win, preferred_element_type=jnp.float32)
    attn_rows = attn_rows.astype(jnp.bfloat16)
    n_head = lax.axis_size("head")
    per_block = routes.shape[0]
    row_start = lax.axis_index("head") * per_block
    leaving = jnp.transpose(attn_rows.reshape(groups, n_head, per_block, head_size), (1, 0, 2, 3))
    arriving = lax.all_to_all(leaving, "head", split_axis=0, concat_axis=0, tiled=True)
    o_weight = o_weight_all.reshape(n_head, groups, head_size, model_width)
    summed = jnp.einsum(
        "hgtc,hgcd->td", arriving, o_weight, preferred_element_type=jnp.float32
    )
    base_rows = lax.dynamic_slice_in_dim(whole, row_start, per_block, 0)
    resid = base_rows.astype(jnp.float32) + summed
    moe_in = norm_rows(resid, norm_moe).astype(jnp.bfloat16)
    capacity = per_block // 2
    expert_ids = jnp.arange(EXPERTS, dtype=jnp.int32)
    onehot = (routes.reshape(-1)[:, None] == expert_ids[None, :]).astype(jnp.bfloat16)
    pair_count = onehot.shape[0]
    chunk = 32
    lower = (
        jnp.arange(chunk, dtype=jnp.int32)[:, None] > jnp.arange(chunk, dtype=jnp.int32)[None, :]
    ).astype(jnp.bfloat16)
    pieces = onehot.reshape(pair_count // chunk, chunk, EXPERTS)
    within = jnp.einsum("ij,cje->cie", lower, pieces, preferred_element_type=jnp.float32)
    piece_total = jnp.sum(pieces.astype(jnp.float32), axis=1)
    piece_lower = (
        jnp.arange(pair_count // chunk, dtype=jnp.int32)[:, None]
        > jnp.arange(pair_count // chunk, dtype=jnp.int32)[None, :]
    ).astype(jnp.float32)
    earlier = jnp.dot(piece_lower, piece_total, precision=lax.Precision.HIGHEST)
    before = (within + earlier[:, None, :]).reshape(pair_count, EXPERTS)
    rank_in = jnp.sum(before * onehot.astype(jnp.float32), axis=1).astype(jnp.int32)
    slot_ids = (routes.reshape(-1) * capacity + rank_in).reshape(per_block, TOPK)
    slot_range = jnp.arange(EXPERTS * capacity, dtype=jnp.int32)
    hits = slot_ids[:, :, None] == slot_range[None, None, :]
    send = jnp.any(hits, axis=1).astype(jnp.bfloat16)
    combine = jnp.sum(jnp.where(hits, route_gain[:, :, None], 0.0), axis=1)
    combine_hi = combine.astype(jnp.bfloat16)
    combine_lo = (combine - combine_hi.astype(jnp.float32)).astype(jnp.bfloat16)
    req_count = lax.axis_size("req")
    per_req = w_down.shape[0]
    ff_width = w_down.shape[1]
    send = send.reshape(per_block, req_count, per_req, capacity)
    combine_hi = combine_hi.reshape(per_block, req_count, per_req, capacity)
    combine_lo = combine_lo.reshape(per_block, req_count, per_req, capacity)
    moe_sum = jnp.zeros((per_block, model_width), jnp.float32)
    for e in range(per_req):
        send_e = send[:, :, e, :].reshape(per_block, req_count * capacity)
        outgoing = lax.dot_general(
            send_e, moe_in, (((0,), (0,)), ((), ())), preferred_element_type=jnp.float32
        ).astype(jnp.bfloat16)
        outgoing = outgoing.reshape(req_count, capacity, model_width)
        landed = lax.all_to_all(outgoing, "req", split_axis=0, concat_axis=0, tiled=True)
        gate_up = jnp.einsum(
            "scd,df->scf", landed, w_gate_up[e], preferred_element_type=jnp.float32
        )
        hidden = (jax.nn.silu(gate_up[..., :ff_width]) * gate_up[..., ff_width:]).astype(
            jnp.bfloat16
        )
        produced = jnp.einsum(
            "scf,fd->scd", hidden, w_down[e], preferred_element_type=jnp.float32
        ).astype(jnp.bfloat16)
        arrived = lax.all_to_all(produced, "req", split_axis=0, concat_axis=0, tiled=True)
        arrived = arrived.reshape(req_count * capacity, model_width)
        hi_e = combine_hi[:, :, e, :].reshape(per_block, req_count * capacity)
        lo_e = combine_lo[:, :, e, :].reshape(per_block, req_count * capacity)
        moe_sum = moe_sum + (
            jnp.dot(hi_e, arrived, preferred_element_type=jnp.float32)
            + jnp.dot(lo_e, arrived, preferred_element_type=jnp.float32)
        )
    return (resid + moe_sum).astype(jnp.bfloat16)


def solution(mesh):
    in_specs = (
        P("req", "head"),
        P("req", None),
        P("req", "head", None, None),
        P(),
        P(None, "head", None),
        P(None, "head", None),
        P("head", None, None),
        P(),
        P(("req", "head"), None),
        P(("req", "head"), None),
        P("req", None, None),
        P("req", None, None),
    )
    out_specs = P(("req", "head"), None)
    return jax.shard_map(local, mesh=mesh, in_specs=in_specs, out_specs=out_specs, check_vma=False)
```

```python
import math

import jax
import jax.numpy as jnp
from jax import lax
from jax.experimental import pallas as pl
from jax.experimental.pallas import tpu as pltpu
from jax.sharding import PartitionSpec as P

EXPERTS = 32
TOPK = 8
RATIO = 15
WIN = 512
TQ = 256
TK = 3840


floor_score = -1e30


def norm_rows(value_rows, gain_row):
    mean_square = jnp.mean(value_rows * value_rows, axis=-1, keepdims=True)
    return value_rows * lax.rsqrt(mean_square + 1e-05) * gain_row


def rope_tables(position, head_size):
    half_size = head_size // 2
    inverse = jnp.exp(
        jnp.arange(half_size, dtype=jnp.float32) * (-2.0 * math.log(10000.0) / head_size)
    )
    angles = position.astype(jnp.float32)[:, None] * inverse[None, :]
    angles = jnp.concatenate([angles, angles], axis=1)
    return (jnp.cos(angles), jnp.sin(angles))


def rotate(vectors, cos_part, sin_part):
    half_size = vectors.shape[-1] // 2
    turned = jnp.concatenate([-vectors[..., half_size:], vectors[..., :half_size]], axis=-1)
    return vectors * cos_part + turned * sin_part


def request_layout(counts, token_count, cache_ratio):
    end_rows = jnp.cumsum(counts)
    starts = end_rows - counts
    row_ids = jnp.arange(token_count, dtype=jnp.int32)
    segment = jnp.sum((row_ids[:, None] >= end_rows[None, :]).astype(jnp.int32), axis=1)
    member = (segment[:, None] == jnp.arange(counts.shape[0], dtype=jnp.int32)[None, :]).astype(
        jnp.int32
    )
    row_begin = jnp.sum(member * starts[None, :], axis=1)
    own_count = jnp.sum(member * counts[None, :], axis=1)
    position = cache_ratio * own_count + row_ids - row_begin
    return (starts, position)


def project(normed, query_weight, key_value_weight, position):
    token_count, model_width = normed.shape
    kv_heads = key_value_weight.shape[1]
    head_size = key_value_weight.shape[2] // 2
    group_size = query_weight.shape[2] // head_size
    query = jnp.dot(
        normed, query_weight.reshape(model_width, -1), preferred_element_type=jnp.float32
    )
    query = query.reshape(token_count, kv_heads, group_size, head_size)
    keyval = jnp.dot(
        normed, key_value_weight.reshape(model_width, -1), preferred_element_type=jnp.float32
    )
    keyval = keyval.reshape(token_count, kv_heads, 2 * head_size)
    cos_part, sin_part = rope_tables(position, head_size)
    query = rotate(query, cos_part[:, None, None, :], sin_part[:, None, None, :])
    query = (query * (1.0 / math.sqrt(head_size))).astype(jnp.bfloat16)
    new_key = rotate(keyval[..., :head_size], cos_part[:, None, :], sin_part[:, None, :]).astype(
        jnp.bfloat16
    )
    new_value = keyval[..., head_size:].astype(jnp.bfloat16)
    return (query, new_key, new_value)


def attn_kernel(counts_ref, q_ref, kv_ref, nkv_ref, o_ref, m_sc, l_sc, acc_sc):
    j = pl.program_id(0)
    qi = pl.program_id(1)
    kb = pl.program_id(2)
    last = pl.num_programs(2) - 1
    count = counts_ref[j]
    cached = RATIO * count
    groups, tq, width = q_ref.shape[0], q_ref.shape[2], q_ref.shape[3]
    tk = kv_ref.shape[2]
    win = nkv_ref.shape[1]
    tile_ok = qi * tq < count

    @pl.when(kb == 0)
    def _():
        m_sc[...] = jnp.full(m_sc.shape, floor_score, jnp.float32)
        l_sc[...] = jnp.zeros(l_sc.shape, jnp.float32)
        acc_sc[...] = jnp.zeros(acc_sc.shape, jnp.float32)

    def absorb(rows, mask):
        q = q_ref[:, 0].reshape(groups * tq, width)
        s = lax.dot_general(
            q, rows, (((1,), (1,)), ((), ())), preferred_element_type=jnp.float32
        )
        s = s.reshape(groups, tq, rows.shape[0])
        if mask is not None:
            s = jnp.where(mask, s, floor_score)
        m_old = m_sc[...]
        m_new = jnp.maximum(m_old, jnp.max(s, axis=-1, keepdims=True))
        alpha = jnp.exp(m_old - m_new)
        p = jnp.exp(s - m_new)
        l_sc[...] = l_sc[...] * alpha + jnp.sum(p, axis=-1, keepdims=True)
        pv = jnp.dot(
            p.astype(jnp.bfloat16).reshape(groups * tq, rows.shape[0]),
            rows,
            preferred_element_type=jnp.float32,
        )
        acc_sc[...] = acc_sc[...] * alpha + pv.reshape(groups, tq, width)
        m_sc[...] = m_new

    @pl.when(tile_ok & (kb == 0))
    def _():
        row = qi * tq + lax.broadcasted_iota(jnp.int32, (1, tq, win), 1)
        col = lax.broadcasted_iota(jnp.int32, (1, tq, win), 2)
        absorb(nkv_ref[0], col <= row)

    @pl.when(tile_ok & (kb > 0) & ((kb - 1) * tk < cached))
    def _():
        col = (kb - 1) * tk + lax.broadcasted_iota(jnp.int32, (1, 1, tk), 2)
        absorb(kv_ref[0, 0], col < cached)

    @pl.when(kb == last)
    def _():
        total = l_sc[...]
        total = jnp.where(total > 0.0, total, 1.0)
        o_ref[:, 0] = (acc_sc[...] / total).astype(o_ref.dtype)


def attention(counts, q_win, kv_cache, nkv_win):
    groups, req_n, win, width = q_win.shape
    cache_len = kv_cache.shape[2]
    n_tiles = win // TQ
    n_blocks = cache_len // TK

    def q_map(j, qi, kb, cnt):
        tiles = (cnt[j] + TQ - 1) // TQ
        return (0, j, jnp.minimum(qi, tiles - 1), 0)

    def kv_map(j, qi, kb, cnt):
        tiles = (cnt[j] + TQ - 1) // TQ
        blocks = (RATIO * cnt[j] + TK - 1) // TK
        inner = jnp.clip(kb - 1, 0, blocks - 1)
        return (j, 0, jnp.where(qi < tiles, inner, blocks - 1), 0)

    grid_spec = pltpu.PrefetchScalarGridSpec(
        num_scalar_prefetch=1,
        grid=(req_n, n_tiles, n_blocks + 1),
        in_specs=[
            pl.BlockSpec((groups, 1, TQ, width), q_map),
            pl.BlockSpec((1, 1, TK, width), kv_map),
            pl.BlockSpec((1, win, width), lambda j, qi, kb, cnt: (j, 0, 0)),
        ],
        out_specs=pl.BlockSpec((groups, 1, TQ, width), lambda j, qi, kb, cnt: (0, j, qi, 0)),
        scratch_shapes=[
            pltpu.VMEM((groups, TQ, 1), jnp.float32),
            pltpu.VMEM((groups, TQ, 1), jnp.float32),
            pltpu.VMEM((groups, TQ, width), jnp.float32),
        ],
    )
    return pl.pallas_call(
        attn_kernel,
        grid_spec=grid_spec,
        out_shape=jax.ShapeDtypeStruct(q_win.shape, jnp.bfloat16),
        compiler_params=pltpu.CompilerParams(
            dimension_semantics=("arbitrary", "arbitrary", "arbitrary")
        ),
    )(counts, q_win, kv_cache, nkv_win)


def turned_columns(weight):
    half = weight.shape[-1] // 2
    return jnp.concatenate([-weight[..., half:], weight[..., :half]], axis=-1)


def local(
    tokens,
    new_counts,
    kv_cache,
    norm_attn,
    query_weight,
    key_value_weight,
    output_weight,
    norm_moe,
    routes,
    route_gain,
    w_gate_up,
    w_down,
):
    whole = lax.all_gather(tokens, "head", axis=1, tiled=True)
    o_weight_all = lax.all_gather(output_weight, "head", axis=0, tiled=True)
    token_count, model_width = whole.shape
    normed = norm_rows(whole.astype(jnp.float32), norm_attn).astype(jnp.bfloat16)
    counts = new_counts[0]
    starts, position = request_layout(counts, token_count, RATIO)
    req_n = counts.shape[0]
    head_size = key_value_weight.shape[2] // 2
    groups = query_weight.shape[2] // head_size
    width = 2 * head_size

    cos_part, sin_part = rope_tables(position, head_size)
    scale = 1.0 / math.sqrt(head_size)
    no_lanes = jnp.zeros((token_count, width - head_size), jnp.float32)
    cos_q = jnp.concatenate([cos_part * scale, no_lanes], axis=1)
    sin_q = jnp.concatenate([sin_part * scale, no_lanes], axis=1)
    q_weight = query_weight.reshape(model_width, groups, head_size)
    no_cols = jnp.zeros((model_width, groups, width - head_size), q_weight.dtype)
    q_plain = jnp.concatenate([q_weight, no_cols], axis=-1)
    q_turned = jnp.concatenate([turned_columns(q_weight), no_cols], axis=-1)
    q_a = jnp.einsum("td,dgc->gtc", normed, q_plain, preferred_element_type=jnp.float32)
    q_b = jnp.einsum("td,dgc->gtc", normed, q_turned, preferred_element_type=jnp.float32)
    query = (q_a * cos_q[None] + q_b * sin_q[None]).astype(jnp.bfloat16)

    kv_weight = key_value_weight.reshape(model_width, width)
    k_turned = jnp.concatenate(
        [turned_columns(kv_weight[:, :head_size]), jnp.zeros_like(kv_weight[:, head_size:])],
        axis=1,
    )
    ones_lanes = jnp.ones((token_count, width - head_size), jnp.float32)
    cos_k = jnp.concatenate([cos_part, ones_lanes], axis=1)
    sin_k = jnp.concatenate([sin_part, no_lanes], axis=1)
    kv_a = jnp.dot(normed, kv_weight, preferred_element_type=jnp.float32)
    kv_b = jnp.dot(normed, k_turned, preferred_element_type=jnp.float32)
    newkv = (kv_a * cos_k + kv_b * sin_k).astype(jnp.bfloat16)

    row_ids = jnp.arange(token_count, dtype=jnp.int32)
    offsets = jnp.arange(WIN, dtype=jnp.int32)
    select = (row_ids[:, None, None] == starts[None, :, None] + offsets[None, None, :]) & (
        offsets[None, None, :] < counts[None, :, None]
    )
    select = select.astype(jnp.bfloat16).reshape(token_count, req_n * WIN)
    q_win = jnp.einsum("tw,gtc->gwc", select, query, preferred_element_type=jnp.float32)
    q_win = q_win.astype(jnp.bfloat16).reshape(groups, req_n, WIN, width)
    nkv_win = jnp.einsum("tw,tc->wc", select, newkv, preferred_element_type=jnp.float32)
    nkv_win = nkv_win.astype(jnp.bfloat16).reshape(req_n, WIN, width)
    out_win = attention(counts, q_win, kv_cache, nkv_win)
    out_win = out_win[..., head_size:].reshape(groups, req_n * WIN, head_size)
    attn_rows = jnp.einsum("tw,gwc->gtc", select, out_win, preferred_element_type=jnp.float32)
    attn_rows = attn_rows.astype(jnp.bfloat16)
    n_head = lax.axis_size("head")
    per_block = routes.shape[0]
    row_start = lax.axis_index("head") * per_block
    leaving = jnp.transpose(attn_rows.reshape(groups, n_head, per_block, head_size), (1, 0, 2, 3))
    arriving = lax.all_to_all(leaving, "head", split_axis=0, concat_axis=0, tiled=True)
    o_weight = o_weight_all.reshape(n_head, groups, head_size, model_width)
    summed = jnp.einsum(
        "hgtc,hgcd->td", arriving, o_weight, preferred_element_type=jnp.float32
    )
    base_rows = lax.dynamic_slice_in_dim(whole, row_start, per_block, 0)
    resid = base_rows.astype(jnp.float32) + summed
    moe_in = norm_rows(resid, norm_moe).astype(jnp.bfloat16)
    capacity = per_block // 2
    expert_ids = jnp.arange(EXPERTS, dtype=jnp.int32)
    onehot = (routes.reshape(-1)[:, None] == expert_ids[None, :]).astype(jnp.bfloat16)
    pair_count = onehot.shape[0]
    chunk = 32
    lower = (
        jnp.arange(chunk, dtype=jnp.int32)[:, None] > jnp.arange(chunk, dtype=jnp.int32)[None, :]
    ).astype(jnp.bfloat16)
    pieces = onehot.reshape(pair_count // chunk, chunk, EXPERTS)
    within = jnp.einsum("ij,cje->cie", lower, pieces, preferred_element_type=jnp.float32)
    piece_total = jnp.sum(pieces.astype(jnp.float32), axis=1)
    piece_lower = (
        jnp.arange(pair_count // chunk, dtype=jnp.int32)[:, None]
        > jnp.arange(pair_count // chunk, dtype=jnp.int32)[None, :]
    ).astype(jnp.float32)
    earlier = jnp.dot(piece_lower, piece_total, precision=lax.Precision.HIGHEST)
    before = (within + earlier[:, None, :]).reshape(pair_count, EXPERTS)
    rank_in = jnp.sum(before * onehot.astype(jnp.float32), axis=1).astype(jnp.int32)
    slot_ids = (routes.reshape(-1) * capacity + rank_in).reshape(per_block, TOPK)
    slot_range = jnp.arange(EXPERTS * capacity, dtype=jnp.int32)
    hits = slot_ids[:, :, None] == slot_range[None, None, :]
    send = jnp.any(hits, axis=1).astype(jnp.bfloat16)
    combine = jnp.sum(jnp.where(hits, route_gain[:, :, None], 0.0), axis=1)
    combine_hi = combine.astype(jnp.bfloat16)
    combine_lo = (combine - combine_hi.astype(jnp.float32)).astype(jnp.bfloat16)
    req_count = lax.axis_size("req")
    per_req = w_down.shape[0]
    ff_width = w_down.shape[1]
    send = send.reshape(per_block, req_count, per_req, capacity)
    combine_hi = combine_hi.reshape(per_block, req_count, per_req, capacity)
    combine_lo = combine_lo.reshape(per_block, req_count, per_req, capacity)
    moe_sum = jnp.zeros((per_block, model_width), jnp.float32)
    for e in range(per_req):
        send_e = send[:, :, e, :].reshape(per_block, req_count * capacity)
        outgoing = lax.dot_general(
            send_e, moe_in, (((0,), (0,)), ((), ())), preferred_element_type=jnp.float32
        ).astype(jnp.bfloat16)
        outgoing = outgoing.reshape(req_count, capacity, model_width)
        landed = lax.all_to_all(outgoing, "req", split_axis=0, concat_axis=0, tiled=True)
        gate_up = jnp.einsum(
            "scd,df->scf", landed, w_gate_up[e], preferred_element_type=jnp.float32
        )
        hidden = (jax.nn.silu(gate_up[..., :ff_width]) * gate_up[..., ff_width:]).astype(
            jnp.bfloat16
        )
        produced = jnp.einsum(
            "scf,fd->scd", hidden, w_down[e], preferred_element_type=jnp.float32
        ).astype(jnp.bfloat16)
        arrived = lax.all_to_all(produced, "req", split_axis=0, concat_axis=0, tiled=True)
        arrived = arrived.reshape(req_count * capacity, model_width)
        hi_e = combine_hi[:, :, e, :].reshape(per_block, req_count * capacity)
        lo_e = combine_lo[:, :, e, :].reshape(per_block, req_count * capacity)
        moe_sum = moe_sum + (
            jnp.dot(hi_e, arrived, preferred_element_type=jnp.float32)
            + jnp.dot(lo_e, arrived, preferred_element_type=jnp.float32)
        )
    return (resid + moe_sum).astype(jnp.bfloat16)


def solution(mesh):
    in_specs = (
        P("req", "head"),
        P("req", None),
        P("req", "head", None, None),
        P(),
        P(None, "head", None),
        P(None, "head", None),
        P("head", None, None),
        P(),
        P(("req", "head"), None),
        P(("req", "head"), None),
        P("req", None, None),
        P("req", None, None),
    )
    out_specs = P(("req", "head"), None)
    return jax.shard_map(local, mesh=mesh, in_specs=in_specs, out_specs=out_specs, check_vma=False)
```

```python
import math

import jax
import jax.numpy as jnp
from jax import lax
from jax.experimental import pallas as pl
from jax.experimental.pallas import tpu as pltpu
from jax.sharding import PartitionSpec as P

EXPERTS = 32
TOPK = 8
RATIO = 15
WIN = 512
TQ = 256
TK = 2560


floor_score = -1e30


def norm_rows(value_rows, gain_row):
    mean_square = jnp.mean(value_rows * value_rows, axis=-1, keepdims=True)
    return value_rows * lax.rsqrt(mean_square + 1e-05) * gain_row


def rope_tables(position, head_size):
    half_size = head_size // 2
    inverse = jnp.exp(
        jnp.arange(half_size, dtype=jnp.float32) * (-2.0 * math.log(10000.0) / head_size)
    )
    angles = position.astype(jnp.float32)[:, None] * inverse[None, :]
    angles = jnp.concatenate([angles, angles], axis=1)
    return (jnp.cos(angles), jnp.sin(angles))


def rotate(vectors, cos_part, sin_part):
    half_size = vectors.shape[-1] // 2
    turned = jnp.concatenate([-vectors[..., half_size:], vectors[..., :half_size]], axis=-1)
    return vectors * cos_part + turned * sin_part


def request_layout(counts, token_count, cache_ratio):
    end_rows = jnp.cumsum(counts)
    starts = end_rows - counts
    row_ids = jnp.arange(token_count, dtype=jnp.int32)
    segment = jnp.sum((row_ids[:, None] >= end_rows[None, :]).astype(jnp.int32), axis=1)
    member = (segment[:, None] == jnp.arange(counts.shape[0], dtype=jnp.int32)[None, :]).astype(
        jnp.int32
    )
    row_begin = jnp.sum(member * starts[None, :], axis=1)
    own_count = jnp.sum(member * counts[None, :], axis=1)
    position = cache_ratio * own_count + row_ids - row_begin
    return (starts, position)


def project(normed, query_weight, key_value_weight, position):
    token_count, model_width = normed.shape
    kv_heads = key_value_weight.shape[1]
    head_size = key_value_weight.shape[2] // 2
    group_size = query_weight.shape[2] // head_size
    query = jnp.dot(
        normed, query_weight.reshape(model_width, -1), preferred_element_type=jnp.float32
    )
    query = query.reshape(token_count, kv_heads, group_size, head_size)
    keyval = jnp.dot(
        normed, key_value_weight.reshape(model_width, -1), preferred_element_type=jnp.float32
    )
    keyval = keyval.reshape(token_count, kv_heads, 2 * head_size)
    cos_part, sin_part = rope_tables(position, head_size)
    query = rotate(query, cos_part[:, None, None, :], sin_part[:, None, None, :])
    query = (query * (1.0 / math.sqrt(head_size))).astype(jnp.bfloat16)
    new_key = rotate(keyval[..., :head_size], cos_part[:, None, :], sin_part[:, None, :]).astype(
        jnp.bfloat16
    )
    new_value = keyval[..., head_size:].astype(jnp.bfloat16)
    return (query, new_key, new_value)


def attn_kernel(counts_ref, q_ref, kv_ref, nkv_ref, o_ref, m_sc, l_sc, acc_sc):
    j = pl.program_id(0)
    qi = pl.program_id(1)
    kb = pl.program_id(2)
    last = pl.num_programs(2) - 1
    count = counts_ref[j]
    cached = RATIO * count
    groups, tq, width = q_ref.shape[0], q_ref.shape[2], q_ref.shape[3]
    tk = kv_ref.shape[2]
    win = nkv_ref.shape[1]
    tile_ok = qi * tq < count

    @pl.when(kb == 0)
    def _():
        m_sc[...] = jnp.full(m_sc.shape, floor_score, jnp.float32)
        l_sc[...] = jnp.zeros(l_sc.shape, jnp.float32)
        acc_sc[...] = jnp.zeros(acc_sc.shape, jnp.float32)

    def absorb(rows, mask):
        q = q_ref[:, 0].reshape(groups * tq, width)
        s = lax.dot_general(
            q, rows, (((1,), (1,)), ((), ())), preferred_element_type=jnp.float32
        )
        s = s.reshape(groups, tq, rows.shape[0])
        if mask is not None:
            s = jnp.where(mask, s, floor_score)
        m_old = m_sc[...]
        m_new = jnp.maximum(m_old, jnp.max(s, axis=-1, keepdims=True))
        alpha = jnp.exp(m_old - m_new)
        p = jnp.exp(s - m_new)
        l_sc[...] = l_sc[...] * alpha + jnp.sum(p, axis=-1, keepdims=True)
        pv = jnp.dot(
            p.astype(jnp.bfloat16).reshape(groups * tq, rows.shape[0]),
            rows,
            preferred_element_type=jnp.float32,
        )
        acc_sc[...] = acc_sc[...] * alpha + pv.reshape(groups, tq, width)
        m_sc[...] = m_new

    @pl.when(tile_ok & (kb == 0) & (qi == 0))
    def _():
        row = lax.broadcasted_iota(jnp.int32, (1, tq, tq), 1)
        col = lax.broadcasted_iota(jnp.int32, (1, tq, tq), 2)
        absorb(nkv_ref[0, :tq, :], col <= row)

    @pl.when(tile_ok & (kb == 0) & (qi > 0))
    def _():
        row = qi * tq + lax.broadcasted_iota(jnp.int32, (1, tq, win), 1)
        col = lax.broadcasted_iota(jnp.int32, (1, tq, win), 2)
        absorb(nkv_ref[0], col <= row)

    @pl.when(tile_ok & (kb > 0) & ((kb - 1) * tk < cached))
    def _():
        col = (kb - 1) * tk + lax.broadcasted_iota(jnp.int32, (1, 1, tk), 2)
        absorb(kv_ref[0, 0], col < cached)

    @pl.when(kb == last)
    def _():
        total = l_sc[...]
        total = jnp.where(total > 0.0, total, 1.0)
        o_ref[:, 0] = (acc_sc[...] / total).astype(o_ref.dtype)


def attention(counts, q_win, kv_cache, nkv_win):
    groups, req_n, win, width = q_win.shape
    cache_len = kv_cache.shape[2]
    n_tiles = win // TQ
    n_blocks = cache_len // TK

    def q_map(j, qi, kb, cnt):
        tiles = (cnt[j] + TQ - 1) // TQ
        return (0, j, jnp.minimum(qi, tiles - 1), 0)

    def kv_map(j, qi, kb, cnt):
        tiles = (cnt[j] + TQ - 1) // TQ
        blocks = (RATIO * cnt[j] + TK - 1) // TK
        inner = jnp.clip(kb - 1, 0, blocks - 1)
        return (j, 0, jnp.where(qi < tiles, inner, blocks - 1), 0)

    grid_spec = pltpu.PrefetchScalarGridSpec(
        num_scalar_prefetch=1,
        grid=(req_n, n_tiles, n_blocks + 1),
        in_specs=[
            pl.BlockSpec((groups, 1, TQ, width), q_map),
            pl.BlockSpec((1, 1, TK, width), kv_map),
            pl.BlockSpec((1, win, width), lambda j, qi, kb, cnt: (j, 0, 0)),
        ],
        out_specs=pl.BlockSpec((groups, 1, TQ, width), lambda j, qi, kb, cnt: (0, j, qi, 0)),
        scratch_shapes=[
            pltpu.VMEM((groups, TQ, 1), jnp.float32),
            pltpu.VMEM((groups, TQ, 1), jnp.float32),
            pltpu.VMEM((groups, TQ, width), jnp.float32),
        ],
    )
    return pl.pallas_call(
        attn_kernel,
        grid_spec=grid_spec,
        out_shape=jax.ShapeDtypeStruct(q_win.shape, jnp.bfloat16),
        compiler_params=pltpu.CompilerParams(
            dimension_semantics=("arbitrary", "arbitrary", "arbitrary")
        ),
    )(counts, q_win, kv_cache, nkv_win)


def turned_columns(weight):
    half = weight.shape[-1] // 2
    return jnp.concatenate([-weight[..., half:], weight[..., :half]], axis=-1)


def local(
    tokens,
    new_counts,
    kv_cache,
    norm_attn,
    query_weight,
    key_value_weight,
    output_weight,
    norm_moe,
    routes,
    route_gain,
    w_gate_up,
    w_down,
):
    whole = lax.all_gather(tokens, "head", axis=1, tiled=True)
    o_weight_all = lax.all_gather(output_weight, "head", axis=0, tiled=True)
    token_count, model_width = whole.shape
    normed = norm_rows(whole.astype(jnp.float32), norm_attn).astype(jnp.bfloat16)
    counts = new_counts[0]
    starts, position = request_layout(counts, token_count, RATIO)
    req_n = counts.shape[0]
    head_size = key_value_weight.shape[2] // 2
    groups = query_weight.shape[2] // head_size
    width = 2 * head_size

    cos_part, sin_part = rope_tables(position, head_size)
    scale = 1.0 / math.sqrt(head_size)
    no_lanes = jnp.zeros((token_count, width - head_size), jnp.float32)
    cos_q = jnp.concatenate([cos_part * scale, no_lanes], axis=1)
    sin_q = jnp.concatenate([sin_part * scale, no_lanes], axis=1)
    q_weight = query_weight.reshape(model_width, groups, head_size)
    no_cols = jnp.zeros((model_width, groups, width - head_size), q_weight.dtype)
    q_plain = jnp.concatenate([q_weight, no_cols], axis=-1)
    q_turned = jnp.concatenate([turned_columns(q_weight), no_cols], axis=-1)
    q_a = jnp.einsum("td,dgc->gtc", normed, q_plain, preferred_element_type=jnp.float32)
    q_b = jnp.einsum("td,dgc->gtc", normed, q_turned, preferred_element_type=jnp.float32)
    query = (q_a * cos_q[None] + q_b * sin_q[None]).astype(jnp.bfloat16)

    kv_weight = key_value_weight.reshape(model_width, width)
    k_turned = jnp.concatenate(
        [turned_columns(kv_weight[:, :head_size]), jnp.zeros_like(kv_weight[:, head_size:])],
        axis=1,
    )
    ones_lanes = jnp.ones((token_count, width - head_size), jnp.float32)
    cos_k = jnp.concatenate([cos_part, ones_lanes], axis=1)
    sin_k = jnp.concatenate([sin_part, no_lanes], axis=1)
    kv_a = jnp.dot(normed, kv_weight, preferred_element_type=jnp.float32)
    kv_b = jnp.dot(normed, k_turned, preferred_element_type=jnp.float32)
    newkv = (kv_a * cos_k + kv_b * sin_k).astype(jnp.bfloat16)

    row_ids = jnp.arange(token_count, dtype=jnp.int32)
    offsets = jnp.arange(WIN, dtype=jnp.int32)
    select = (row_ids[:, None, None] == starts[None, :, None] + offsets[None, None, :]) & (
        offsets[None, None, :] < counts[None, :, None]
    )
    select = select.astype(jnp.bfloat16).reshape(token_count, req_n * WIN)
    q_win = jnp.einsum("tw,gtc->gwc", select, query, preferred_element_type=jnp.float32)
    q_win = q_win.astype(jnp.bfloat16).reshape(groups, req_n, WIN, width)
    nkv_win = jnp.einsum("tw,tc->wc", select, newkv, preferred_element_type=jnp.float32)
    nkv_win = nkv_win.astype(jnp.bfloat16).reshape(req_n, WIN, width)
    out_win = attention(counts, q_win, kv_cache, nkv_win)
    out_win = out_win[..., head_size:].reshape(groups, req_n * WIN, head_size)
    attn_rows = jnp.einsum("tw,gwc->gtc", select, out_win, preferred_element_type=jnp.float32)
    attn_rows = attn_rows.astype(jnp.bfloat16)
    n_head = lax.axis_size("head")
    per_block = routes.shape[0]
    row_start = lax.axis_index("head") * per_block
    leaving = jnp.transpose(attn_rows.reshape(groups, n_head, per_block, head_size), (1, 0, 2, 3))
    arriving = lax.all_to_all(leaving, "head", split_axis=0, concat_axis=0, tiled=True)
    o_weight = o_weight_all.reshape(n_head, groups, head_size, model_width)
    summed = jnp.einsum(
        "hgtc,hgcd->td", arriving, o_weight, preferred_element_type=jnp.float32
    )
    base_rows = lax.dynamic_slice_in_dim(whole, row_start, per_block, 0)
    resid = base_rows.astype(jnp.float32) + summed
    moe_in = norm_rows(resid, norm_moe).astype(jnp.bfloat16)
    capacity = per_block // 2
    expert_ids = jnp.arange(EXPERTS, dtype=jnp.int32)
    onehot = (routes.reshape(-1)[:, None] == expert_ids[None, :]).astype(jnp.bfloat16)
    pair_count = onehot.shape[0]
    chunk = 32
    lower = (
        jnp.arange(chunk, dtype=jnp.int32)[:, None] > jnp.arange(chunk, dtype=jnp.int32)[None, :]
    ).astype(jnp.bfloat16)
    pieces = onehot.reshape(pair_count // chunk, chunk, EXPERTS)
    within = jnp.einsum("ij,cje->cie", lower, pieces, preferred_element_type=jnp.float32)
    piece_total = jnp.sum(pieces.astype(jnp.float32), axis=1)
    piece_lower = (
        jnp.arange(pair_count // chunk, dtype=jnp.int32)[:, None]
        > jnp.arange(pair_count // chunk, dtype=jnp.int32)[None, :]
    ).astype(jnp.float32)
    earlier = jnp.dot(piece_lower, piece_total, precision=lax.Precision.HIGHEST)
    before = (within + earlier[:, None, :]).reshape(pair_count, EXPERTS)
    rank_in = jnp.sum(before * onehot.astype(jnp.float32), axis=1).astype(jnp.int32)
    slot_ids = (routes.reshape(-1) * capacity + rank_in).reshape(per_block, TOPK)
    slot_range = jnp.arange(EXPERTS * capacity, dtype=jnp.int32)
    hits = slot_ids[:, :, None] == slot_range[None, None, :]
    send = jnp.any(hits, axis=1).astype(jnp.bfloat16)
    combine = jnp.sum(jnp.where(hits, route_gain[:, :, None], 0.0), axis=1)
    combine_hi = combine.astype(jnp.bfloat16)
    combine_lo = (combine - combine_hi.astype(jnp.float32)).astype(jnp.bfloat16)
    req_count = lax.axis_size("req")
    per_req = w_down.shape[0]
    ff_width = w_down.shape[1]
    send = send.reshape(per_block, req_count, per_req, capacity)
    combine_hi = combine_hi.reshape(per_block, req_count, per_req, capacity)
    combine_lo = combine_lo.reshape(per_block, req_count, per_req, capacity)
    moe_sum = jnp.zeros((per_block, model_width), jnp.float32)
    for e in range(per_req):
        send_e = send[:, :, e, :].reshape(per_block, req_count * capacity)
        outgoing = lax.dot_general(
            send_e, moe_in, (((0,), (0,)), ((), ())), preferred_element_type=jnp.float32
        ).astype(jnp.bfloat16)
        outgoing = outgoing.reshape(req_count, capacity, model_width)
        landed = lax.all_to_all(outgoing, "req", split_axis=0, concat_axis=0, tiled=True)
        gate_up = jnp.einsum(
            "scd,df->scf", landed, w_gate_up[e], preferred_element_type=jnp.float32
        )
        hidden = (jax.nn.silu(gate_up[..., :ff_width]) * gate_up[..., ff_width:]).astype(
            jnp.bfloat16
        )
        produced = jnp.einsum(
            "scf,fd->scd", hidden, w_down[e], preferred_element_type=jnp.float32
        ).astype(jnp.bfloat16)
        arrived = lax.all_to_all(produced, "req", split_axis=0, concat_axis=0, tiled=True)
        arrived = arrived.reshape(req_count * capacity, model_width)
        hi_e = combine_hi[:, :, e, :].reshape(per_block, req_count * capacity)
        lo_e = combine_lo[:, :, e, :].reshape(per_block, req_count * capacity)
        moe_sum = moe_sum + (
            jnp.dot(hi_e, arrived, preferred_element_type=jnp.float32)
            + jnp.dot(lo_e, arrived, preferred_element_type=jnp.float32)
        )
    return (resid + moe_sum).astype(jnp.bfloat16)


def solution(mesh):
    in_specs = (
        P("req", "head"),
        P("req", None),
        P("req", "head", None, None),
        P(),
        P(None, "head", None),
        P(None, "head", None),
        P("head", None, None),
        P(),
        P(("req", "head"), None),
        P(("req", "head"), None),
        P("req", None, None),
        P("req", None, None),
    )
    out_specs = P(("req", "head"), None)
    return jax.shard_map(local, mesh=mesh, in_specs=in_specs, out_specs=out_specs, check_vma=False)
```
